128 devices in a mesh: req: 32 (over x, z, core), seq: 4 (over y).
Axes of the slice: x: 4, y: 4, z: 4, core: 2. Of those that a mesh axis runs over, the one named last changes fastest.
Arguments:
- xs: bfloat16 [16384, 8192], P(('req', 'seq')), may hold values from -6 to 6
- bc: bfloat16 [16384, 2048], P(('req', 'seq')), may hold values from -6 to 6
- zgate: bfloat16 [16384, 8192], P(('req', 'seq'))
- dt_raw: bfloat16 [16384, 128], P(('req', 'seq'))
- dt_bias: float32 [128], replicated
- a_log: float32 [128], replicated, may hold values from -0.5 to 1
- d_skip: float32 [128], replicated, may hold values from 0.5 to 1.5
- norm_gain: float32 [8192], replicated, may hold values from 0.1 to 1.9
- resid: bfloat16 [16384, 4096], P('req', 'seq')
- w_out: bfloat16 [8192, 4096], P('req'), may hold values from -0.0625 to 0.0625
- final_gain: float32 [4096], replicated, may hold values from 0.1 to 1.9
- head_weight: bfloat16 [4096, 32768], P(None, ('req', 'seq')), may hold values from -0.09375 to 0.09375
- lengths: int32 [32, 2], P('req'), may hold values from 1 to 511, as said below
Outputs:
- layer_out: bfloat16 [16384, 4096], P('req', 'seq')
- logits: float32 [64, 32768], P(None, ('req', 'seq'))
The draws below stay inside these ranges and needn't reach their ends.
Inputs may be any that keep to these rules, and one draw needn't show every extreme that they name: Every request has at least one row; a group's lengths sum to at most 512, and to exactly 512 in at least two groups, where one request takes all but 2 - 1 rows.
All inputs are finite; a program needn't handle non-finite values.
Results may differ from the reference program's by a relative error of at most 0.013.
Values may be sent and summed in bfloat16 or wider, within the bound.
No kernel may reach another device: no remote copies, remote signals or barrier semaphores. Data moves between devices by JAX's collectives and lax.ppermute only.
A program may use at most 128 MiB of HBM per device.

```python
import math
import jax
import jax.numpy as jnp
from jax import lax

D = 4096
SSM_CHANNEL_COUNT = 128
HEAD_DIM = 64
NGROUPS = 8
STATE = 128
VOCAB = 32768
TOK_DEV = 128
SLOTS = 2
INNER = 8192
BCW = 2048
OWNERS = 32
GROUP_TOK = 512
PACKED_LENGTH = 16384
REQS = 64
N_SEQ = 4


def draw_lengths(key, part):
    key_short = jax.random.fold_in(key, 11)
    key_pick = jax.random.fold_in(key, 12)
    groups = REQS // SLOTS
    short = jax.random.randint(key_short, (groups, SLOTS), 1, GROUP_TOK // SLOTS + 1)
    order = jax.random.permutation(key_pick, groups)
    chosen = (order < 2)[:, None]
    slot_index = jnp.arange(SLOTS, dtype=jnp.int32)
    long_row = jnp.where(slot_index == 0, GROUP_TOK - SLOTS + 1, 1)
    return jnp.where(chosen, long_row[None, :], short).astype(jnp.int32)


def draw_dt_raw(key, part):
    key_base = jax.random.fold_in(key, 21)
    sampler_seed_handle = jax.random.fold_in(key, 22)
    starting_entry = 0.6 * jax.random.normal(key_base, (PACKED_LENGTH, SSM_CHANNEL_COUNT), jnp.float32)
    sample_group_entries = (jax.random.uniform(sampler_seed_handle, (PACKED_LENGTH, SSM_CHANNEL_COUNT), jnp.float32) < 0.005).astype(jnp.float32)
    return (starting_entry + 6.0 * sample_group_entries).astype(jnp.bfloat16)


def draw_dt_bias(key, part):
    key_bias = jax.random.fold_in(key, 31)
    return jax.random.uniform(key_bias, (SSM_CHANNEL_COUNT,), jnp.float32, -6.0, -2.5)


def draw_resid(key, part):
    key_row = jax.random.fold_in(key, 41)
    key_col = jax.random.fold_in(key, 42)
    key_base = jax.random.fold_in(key, 43)
    low = math.log(0.32)
    high = math.log(3.16)
    row_scale = jnp.exp(jax.random.uniform(key_row, (PACKED_LENGTH, 1), jnp.float32, low, high))
    col_scale = jnp.exp(jax.random.uniform(key_col, (1, D), jnp.float32, low, high))
    starting_entry = jax.random.normal(key_base, (PACKED_LENGTH, D), jnp.float32)
    return (starting_entry * row_scale * col_scale).astype(jnp.bfloat16)


def draw_zgate(key, part):
    key_col = jax.random.fold_in(key, 51)
    key_base = jax.random.fold_in(key, 52)
    col_scale = jnp.exp(jax.random.uniform(key_col, (1, INNER), jnp.float32, math.log(0.5), math.log(5.0)))
    starting_entry = jax.random.normal(key_base, (PACKED_LENGTH, INNER), jnp.float32)
    return (starting_entry * col_scale).astype(jnp.bfloat16)


def shard_levels(own_key, extent, pieces, least, high):
    factor_of, own = 1.0, jax.random.fold_in(own_key, 6)
    for position, parts in pieces:
        draws = jnp.exp(jax.random.uniform(jax.random.fold_in(own, position), (parts,), jnp.float32, least / len(pieces), high / len(pieces)))
        factor_of = factor_of * jnp.repeat(draws, extent[position] // parts).reshape([-1 if axis == position else 1 for axis in range(len(extent))])
    return factor_of


def centred(stream_key, shape, width, limit, shards=(), held_as=jnp.bfloat16):
    values = jax.random.normal(stream_key, shape, jnp.float32) * width
    if len(shards) > 0:
        values = shard_levels(stream_key, shape, shards, -0.22, 0.18) * values
    return jnp.clip(values, min=-limit, max=limit).astype(held_as)


def setup_inputs(seed: int = 0) -> dict:
    splits = jax.random.split(jax.random.key(seed), 14)
    xs = centred(splits[0], (PACKED_LENGTH, INNER), 1.0, 6.0, ((0, 128),))
    bc = centred(splits[1], (PACKED_LENGTH, BCW), 1.0, 6.0, ((0, 128),))
    zgate = draw_zgate(jax.random.fold_in(splits[13], 71), 0)
    dt_raw = draw_dt_raw(jax.random.fold_in(splits[13], 71), 0)
    dt_bias = draw_dt_bias(jax.random.fold_in(splits[13], 71), 0)
    a_log = jnp.clip(jax.random.uniform(splits[5], (SSM_CHANNEL_COUNT,), jnp.float32, -0.5, 1.0), -0.5, 1.0)
    d_skip = jnp.clip(jax.random.uniform(splits[6], (SSM_CHANNEL_COUNT,), jnp.float32, 0.5, 1.5), 0.5, 1.5)
    norm_gain = jnp.clip(1.0 + 0.18 * jax.random.normal(splits[7], (INNER,), jnp.float32), 0.1, 1.9)
    resid = draw_resid(jax.random.fold_in(splits[13], 71), 0)
    w_out = centred(splits[9], (INNER, D), INNER ** -0.5, 0.0625, ((0, 32),))
    final_gain = jnp.clip(1.0 + 0.18 * jax.random.normal(splits[10], (D,), jnp.float32), 0.1, 1.9)
    head_weight = centred(splits[11], (D, VOCAB), D ** -0.5, 0.09375, ((1, 128),))
    lengths = draw_lengths(jax.random.fold_in(splits[13], 71), 0)
    return dict(xs=xs, bc=bc, zgate=zgate, dt_raw=dt_raw, dt_bias=dt_bias, a_log=a_log, d_skip=d_skip, norm_gain=norm_gain, resid=resid, w_out=w_out, final_gain=final_gain, head_weight=head_weight, lengths=lengths)


HIGH = lax.Precision.HIGHEST

def block_terms(xb, bcb, dtb, segment, live, prev_seg, rate, d_skip):
    rows = xb.shape[0]
    per_group = SSM_CHANNEL_COUNT // NGROUPS
    x4 = xb.astype(jnp.float32).reshape(rows, NGROUPS, per_group, HEAD_DIM)
    bmat = bcb[:, :NGROUPS * STATE].astype(jnp.float32).reshape(rows, NGROUPS, STATE)
    cmat = bcb[:, NGROUPS * STATE:].astype(jnp.float32).reshape(rows, NGROUPS, STATE)
    livef = live.astype(jnp.float32)
    cum = jnp.cumsum(-rate[None, :] * dtb, axis=0)
    inflow = dtb * livef[:, None]
    index = jnp.arange(rows, dtype=jnp.int32)
    allowed_mask = (segment[:, None] == segment[None, :]) & (index[:, None] >= index[None, :])
    diff = cum[:, None, :] - cum[None, :, :]
    decay = jnp.where(allowed_mask[:, :, None], jnp.exp(jnp.minimum(diff, 0.0)), 0.0)
    scores = jnp.einsum('tgn,sgn->tsg', cmat, bmat, precision=HIGH)
    weights = decay.reshape(rows, rows, NGROUPS, per_group) * scores[:, :, :, None] * inflow.reshape(1, rows, NGROUPS, per_group)
    y_inner = jnp.einsum('tsgk,sgkp->tgkp', weights, x4, precision=HIGH)
    skip = d_skip.reshape(1, NGROUPS, per_group, 1) * x4
    last_seg = segment[rows - 1]
    tail = jnp.exp(cum[rows - 1][None, :] - cum) * (segment == last_seg).astype(jnp.float32)[:, None] * inflow
    state = jnp.einsum('sgkp,sgn->gkpn', tail.reshape(rows, NGROUPS, per_group, 1) * x4, bmat, precision=HIGH)
    keep = jnp.exp(cum[rows - 1]) * (last_seg == prev_seg).astype(jnp.float32)
    carry_w = jnp.exp(cum) * (segment == prev_seg).astype(jnp.float32)[:, None]
    return (y_inner + skip, keep, state.reshape(SSM_CHANNEL_COUNT, HEAD_DIM, STATE), carry_w, cmat)

def carry_term(arriving_vector, cmat, carry_w):
    rows = cmat.shape[0]
    per_group = SSM_CHANNEL_COUNT // NGROUPS
    state4 = arriving_vector.reshape(NGROUPS, per_group, HEAD_DIM, STATE)
    y_carry = jnp.einsum('tgn,gkpn->tgkp', cmat, state4, precision=HIGH)
    return y_carry * carry_w.reshape(rows, NGROUPS, per_group, 1)

def gate_norm(y, zgate, norm_gain):
    rows = y.shape[0]
    gated = y * jax.nn.silu(zgate.astype(jnp.float32))
    blocks = gated.reshape(rows, NGROUPS, -1)
    meansq = lax.optimization_barrier(jnp.mean(blocks * blocks, axis=-1, keepdims=True))
    normed = (blocks * lax.rsqrt(meansq + 1e-05)).reshape(rows, -1) * norm_gain[None, :]
    return normed.astype(jnp.bfloat16)

def reference(xs, bc, zgate, dt_raw, dt_bias, a_log, d_skip, norm_gain, resid, w_out, final_gain, head_weight, lengths):
    rate = jnp.exp(a_log)
    dt_all = jax.nn.softplus(dt_raw.astype(jnp.float32) + dt_bias[None, :])

    def one_group(group_args):
        xg, bg, zg, dg, lens = group_args
        ends = jnp.cumsum(lens).astype(jnp.int32)
        positions = jnp.arange(GROUP_TOK, dtype=jnp.int32)
        segment = lax.optimization_barrier(jnp.sum((positions[:, None] >= ends[None, :]).astype(jnp.int32), axis=1)).astype(jnp.int32)
        live = segment < SLOTS

        def progress_update(carry, block):
            state_in, prev_seg = carry
            xb, bb, db, sb, lb = block
            local, keep, state, carry_w, cmat = block_terms(xb, bb, db, sb, lb, prev_seg, rate, d_skip)
            y4 = (local + carry_term(state_in, cmat, carry_w)) * lb.astype(jnp.float32)[:, None, None, None]
            new_state = keep[:, None, None] * state_in + state
            return ((new_state, sb[TOK_DEV - 1]), y4.reshape(TOK_DEV, INNER))
        init = (jnp.zeros((SSM_CHANNEL_COUNT, HEAD_DIM, STATE), jnp.float32), jnp.array(-1, dtype=jnp.int32))
        blocks = (xg.reshape(N_SEQ, TOK_DEV, INNER), bg.reshape(N_SEQ, TOK_DEV, BCW), dg.reshape(N_SEQ, TOK_DEV, SSM_CHANNEL_COUNT), segment.reshape(N_SEQ, TOK_DEV), live.reshape(N_SEQ, TOK_DEV))
        _, ys = lax.scan(progress_update, init, blocks)
        gated = gate_norm(ys.reshape(GROUP_TOK, INNER), zg, norm_gain)
        return jnp.dot(gated, w_out, preferred_element_type=jnp.float32).astype(jnp.bfloat16)
    mixer = lax.map(one_group, (xs.reshape(OWNERS, GROUP_TOK, INNER), bc.reshape(OWNERS, GROUP_TOK, BCW), zgate.reshape(OWNERS, GROUP_TOK, INNER), dt_all.reshape(OWNERS, GROUP_TOK, SSM_CHANNEL_COUNT), lengths))
    layer_out = (resid.astype(jnp.float32) + mixer.reshape(PACKED_LENGTH, D).astype(jnp.float32)).astype(jnp.bfloat16)
    starts = jnp.arange(OWNERS, dtype=jnp.int32)[:, None] * GROUP_TOK
    last_pos = (starts + jnp.cumsum(lengths, axis=1).astype(jnp.int32) - 1).reshape(-1).astype(jnp.int32)
    last_rows = jnp.take(layer_out, last_pos, axis=0).astype(jnp.float32)
    meansq = lax.optimization_barrier(jnp.mean(last_rows * last_rows, axis=-1, keepdims=True))
    normed = (last_rows * lax.rsqrt(meansq + 1e-05) * final_gain[None, :]).astype(jnp.bfloat16)
    logits = jnp.dot(normed, head_weight, preferred_element_type=jnp.float32)
    return (layer_out, logits)
```

```python
import jax
import jax.numpy as jnp
from jax import lax
from jax.sharding import PartitionSpec as P

SSM_CHANNEL_COUNT = 128
HEAD_DIM = 64
NGROUPS = 8
STATE = 128


def split_halves(value):
    upper = value.astype(jnp.bfloat16)
    lower = (value - upper.astype(jnp.float32)).astype(jnp.bfloat16)
    return (upper, lower)


def group_inner(operands):
    cum_g, scores_g, inflow_g, x_g, allowed_mask = operands
    diff = cum_g[:, None, :] - cum_g[None, :, :]
    decay = jnp.where(allowed_mask[:, :, None], jnp.exp(jnp.minimum(diff, 0.0)), 0.0)
    weights = decay * scores_g[:, :, None] * inflow_g[None, :, :]
    upper, lower = split_halves(weights)
    first_part = jnp.einsum("tsk,skp->tkp", upper, x_g, preferred_element_type=jnp.float32)
    second_part = jnp.einsum("tsk,skp->tkp", lower, x_g, preferred_element_type=jnp.float32)
    return first_part + second_part


def block_terms(xb, bb, cb, dtb, segment, live, prev_seg, rate, d_skip, groups):
    rows = xb.shape[0]
    heads = rate.shape[0]
    per_group = heads // groups
    x4 = xb.reshape(rows, groups, per_group, HEAD_DIM)
    bmat = bb.reshape(rows, groups, STATE)
    cmat = cb.reshape(rows, groups, STATE)
    livef = live.astype(jnp.float32)
    cum = jnp.cumsum(-rate[None, :] * dtb, axis=0)
    inflow = dtb * livef[:, None]
    index = jnp.arange(rows, dtype=jnp.int32)
    allowed_mask = (segment[:, None] == segment[None, :]) & (index[:, None] >= index[None, :])
    scores = jnp.einsum("tgn,sgn->gts", cmat, bmat, preferred_element_type=jnp.float32)
    cum_g = cum.reshape(rows, groups, per_group).transpose(1, 0, 2)
    inflow_g = inflow.reshape(rows, groups, per_group).transpose(1, 0, 2)
    x_g = x4.transpose(1, 0, 2, 3)
    allowed_all = jnp.broadcast_to(allowed_mask[None], (groups, rows, rows))
    y_groups = lax.map(group_inner, (cum_g, scores, inflow_g, x_g, allowed_all))
    y_inner = y_groups.transpose(1, 0, 2, 3)
    skip = d_skip.reshape(1, groups, per_group, 1) * x4.astype(jnp.float32)
    last_seg = segment[rows - 1]
    tail = (
        jnp.exp(cum[rows - 1][None, :] - cum)
        * (segment == last_seg).astype(jnp.float32)[:, None]
        * inflow
    )
    scaled = tail.reshape(rows, groups, per_group, 1) * x4.astype(jnp.float32)
    upper, lower = split_halves(scaled)
    state = jnp.einsum("sgkp,sgn->gkpn", upper, bmat, preferred_element_type=jnp.float32)
    state = state + jnp.einsum("sgkp,sgn->gkpn", lower, bmat, preferred_element_type=jnp.float32)
    keep = jnp.exp(cum[rows - 1]) * (last_seg == prev_seg).astype(jnp.float32)
    carry_w = jnp.exp(cum) * (segment == prev_seg).astype(jnp.float32)[:, None]
    return (y_inner + skip, keep, state.reshape(heads, HEAD_DIM, STATE), carry_w, cmat)


def carry_term(arriving_vector, cmat, carry_w, groups):
    rows = cmat.shape[0]
    heads = arriving_vector.shape[0]
    per_group = heads // groups
    state4 = arriving_vector.reshape(groups, per_group, HEAD_DIM, STATE)
    upper, lower = split_halves(state4)
    y_carry = jnp.einsum("tgn,gkpn->tgkp", cmat, upper, preferred_element_type=jnp.float32)
    y_carry = y_carry + jnp.einsum(
        "tgn,gkpn->tgkp", cmat, lower, preferred_element_type=jnp.float32
    )
    return y_carry * carry_w.reshape(rows, groups, per_group, 1)


def gate_norm(y, zgate, norm_gain, groups):
    rows = y.shape[0]
    gated = y * jax.nn.silu(zgate.astype(jnp.float32))
    blocks = gated.reshape(rows, groups, -1)
    meansq = jnp.mean(blocks * blocks, axis=-1, keepdims=True)
    normed = (blocks * lax.rsqrt(meansq + 1e-05)).reshape(rows, -1) * norm_gain[None, :]
    return normed.astype(jnp.bfloat16)


def on_device(
    xs,
    bc,
    zgate,
    dt_raw,
    dt_bias,
    a_log,
    d_skip,
    norm_gain,
    resid,
    w_out,
    final_gain,
    head_weight,
    lengths,
):
    rows = xs.shape[0]
    inner = xs.shape[1]
    seq_count = lax.axis_size("seq")
    place = lax.axis_index("seq")
    heads_all = a_log.shape[0]
    heads = heads_all // seq_count
    groups = NGROUPS // seq_count
    share = inner // seq_count
    bshare = groups * STATE
    group_rows = rows * seq_count

    bpart = bc[:, : NGROUPS * STATE].reshape(rows, seq_count, bshare)
    cpart = bc[:, NGROUPS * STATE :].reshape(rows, seq_count, bshare)
    packed = jnp.concatenate(
        [
            xs.reshape(rows, seq_count, share),
            zgate.reshape(rows, seq_count, share),
            bpart,
            cpart,
            dt_raw.reshape(rows, seq_count, heads),
        ],
        axis=2,
    )
    moved = lax.all_to_all(packed, "seq", split_axis=1, concat_axis=0, tiled=True)
    moved = moved.reshape(group_rows, -1)
    xg = moved[:, :share]
    zg = moved[:, share : 2 * share]
    bg = moved[:, 2 * share : 2 * share + bshare]
    cg = moved[:, 2 * share + bshare : 2 * share + 2 * bshare]
    dg = moved[:, 2 * share + 2 * bshare :]

    my_heads = lambda v: lax.dynamic_slice_in_dim(v, place * heads, heads)
    rate = jnp.exp(my_heads(a_log))
    skipw = my_heads(d_skip)
    steps_dt = jax.nn.softplus(dg.astype(jnp.float32) + my_heads(dt_bias)[None, :])

    lens = lengths[0]
    slots = lens.shape[0]
    ends = jnp.cumsum(lens)
    positions = jnp.arange(group_rows, dtype=jnp.int32)
    segment = jnp.sum((positions[:, None] >= ends[None, :]).astype(jnp.int32), axis=1)
    live = segment < slots

    state_in = jnp.zeros((heads, HEAD_DIM, STATE), jnp.float32)
    prev_seg = jnp.array(-1, jnp.int32)
    ys = []
    for chunk in range(seq_count):
        lo, hi = chunk * rows, (chunk + 1) * rows
        local, keep, state, carry_w, cmat = block_terms(
            xg[lo:hi], bg[lo:hi], cg[lo:hi], steps_dt[lo:hi], segment[lo:hi], live[lo:hi],
            prev_seg, rate, skipw, groups,
        )
        y4 = (local + carry_term(state_in, cmat, carry_w, groups)) * live[lo:hi].astype(
            jnp.float32
        )[:, None, None, None]
        ys.append(y4.reshape(rows, share))
        state_in = keep[:, None, None] * state_in + state
        prev_seg = segment[hi - 1]
    y = jnp.concatenate(ys, axis=0)
    gain = lax.dynamic_slice_in_dim(norm_gain, place * share, share)
    gated = gate_norm(y, zg, gain, groups)

    width = resid.shape[1]
    w_cols = lax.dynamic_slice_in_dim(w_out, place * width, width, axis=1)
    w_full = lax.all_gather(w_cols, "req", axis=0, tiled=True)
    gated_all = lax.all_gather(gated, "seq", axis=1, tiled=True)
    mixer = jnp.dot(gated_all, w_full, preferred_element_type=jnp.float32).astype(jnp.bfloat16)
    layer_out = (resid.astype(jnp.float32) + mixer.astype(jnp.float32)).astype(jnp.bfloat16)

    group_pos = jnp.arange(group_rows, dtype=jnp.int32)
    picker = (group_pos[None, :] == (ends - 1)[:, None]).astype(jnp.bfloat16)
    picked_rows = jnp.dot(picker, layer_out, preferred_element_type=jnp.float32).astype(
        jnp.bfloat16
    )
    collected = lax.all_gather(picked_rows, ("req", "seq"), axis=0, tiled=True)
    owners_all = collected.shape[0] // (seq_count * slots)
    last_rows = collected.reshape(owners_all, seq_count, slots, width).transpose(0, 2, 1, 3)
    last_rows = last_rows.reshape(owners_all * slots, seq_count * width).astype(jnp.float32)
    meansq = jnp.mean(last_rows * last_rows, axis=-1, keepdims=True)
    normed = (last_rows * lax.rsqrt(meansq + 1e-05) * final_gain[None, :]).astype(jnp.bfloat16)
    logits = jnp.dot(normed, head_weight, preferred_element_type=jnp.float32)
    return (layer_out, logits)


def solution(mesh):
    placed = (
        P(("req", "seq"), None),
        P(("req", "seq"), None),
        P(("req", "seq"), None),
        P(("req", "seq"), None),
        P(),
        P(),
        P(),
        P(),
        P("req", "seq"),
        P("req", None),
        P(),
        P(None, ("req", "seq")),
        P("req", None),
    )
    return jax.shard_map(
        on_device,
        mesh=mesh,
        in_specs=placed,
        out_specs=(P("req", "seq"), P(None, ("req", "seq"))),
        check_vma=False,
    )
```

```python
import jax
import jax.numpy as jnp
from jax import lax
from jax.sharding import PartitionSpec as P

HEAD_DIM = 64
NGROUPS = 8
STATE = 128


def split_halves(value):
    upper = value.astype(jnp.bfloat16)
    lower = (value - upper.astype(jnp.float32)).astype(jnp.bfloat16)
    return (upper, lower)


def group_inner(operands):
    cum_g, scores_g, inflow_g, x_g, allowed_mask = operands
    diff = cum_g[:, None, :] - cum_g[None, :, :]
    decay = jnp.where(allowed_mask[:, :, None], jnp.exp(jnp.minimum(diff, 0.0)), 0.0)
    weights = decay * scores_g[:, :, None] * inflow_g[None, :, :]
    upper, lower = split_halves(weights)
    first_part = jnp.einsum("tsk,skp->tkp", upper, x_g, preferred_element_type=jnp.float32)
    second_part = jnp.einsum("tsk,skp->tkp", lower, x_g, preferred_element_type=jnp.float32)
    return first_part + second_part


def block_terms(xb, bb, cb, dtb, segment, live, prev_seg, rate, d_skip, groups):
    rows = xb.shape[0]
    heads = rate.shape[0]
    per_group = heads // groups
    x4 = xb.reshape(rows, groups, per_group, HEAD_DIM)
    bmat = bb.reshape(rows, groups, STATE)
    cmat = cb.reshape(rows, groups, STATE)
    livef = live.astype(jnp.float32)
    cum = jnp.cumsum(-rate[None, :] * dtb, axis=0)
    inflow = dtb * livef[:, None]
    index = jnp.arange(rows, dtype=jnp.int32)
    allowed_mask = (segment[:, None] == segment[None, :]) & (index[:, None] >= index[None, :])
    scores = jnp.einsum("tgn,sgn->gts", cmat, bmat, preferred_element_type=jnp.float32)
    cum_g = cum.reshape(rows, groups, per_group).transpose(1, 0, 2)
    inflow_g = inflow.reshape(rows, groups, per_group).transpose(1, 0, 2)
    x_g = x4.transpose(1, 0, 2, 3)
    allowed_all = jnp.broadcast_to(allowed_mask[None], (groups, rows, rows))
    y_groups = lax.map(group_inner, (cum_g, scores, inflow_g, x_g, allowed_all))
    y_inner = y_groups.transpose(1, 0, 2, 3)
    skip = d_skip.reshape(1, groups, per_group, 1) * x4.astype(jnp.float32)
    last_seg = segment[rows - 1]
    tail = (
        jnp.exp(cum[rows - 1][None, :] - cum)
        * (segment == last_seg).astype(jnp.float32)[:, None]
        * inflow
    )
    scaled = tail.reshape(rows, groups, per_group, 1) * x4.astype(jnp.float32)
    upper, lower = split_halves(scaled)
    state = jnp.einsum("sgkp,sgn->gkpn", upper, bmat, preferred_element_type=jnp.float32)
    state = state + jnp.einsum("sgkp,sgn->gkpn", lower, bmat, preferred_element_type=jnp.float32)
    keep = jnp.exp(cum[rows - 1]) * (last_seg == prev_seg).astype(jnp.float32)
    carry_w = jnp.exp(cum) * (segment == prev_seg).astype(jnp.float32)[:, None]
    return (y_inner + skip, keep, state.reshape(heads, HEAD_DIM, STATE), carry_w, cmat)


def carry_term(arriving_vector, cmat, carry_w, groups):
    rows = cmat.shape[0]
    heads = arriving_vector.shape[0]
    per_group = heads // groups
    state4 = arriving_vector.reshape(groups, per_group, HEAD_DIM, STATE)
    upper, lower = split_halves(state4)
    y_carry = jnp.einsum("tgn,gkpn->tgkp", cmat, upper, preferred_element_type=jnp.float32)
    y_carry = y_carry + jnp.einsum(
        "tgn,gkpn->tgkp", cmat, lower, preferred_element_type=jnp.float32
    )
    return y_carry * carry_w.reshape(rows, groups, per_group, 1)


def gate_norm(y, zgate, norm_gain, groups):
    rows = y.shape[0]
    gated = y * jax.nn.silu(zgate.astype(jnp.float32))
    blocks = gated.reshape(rows, groups, -1)
    meansq = jnp.mean(blocks * blocks, axis=-1, keepdims=True)
    normed = (blocks * lax.rsqrt(meansq + 1e-05)).reshape(rows, -1) * norm_gain[None, :]
    return normed.astype(jnp.bfloat16)


def mixer_layer(
    xs,
    bc,
    zgate,
    dt_raw,
    dt_bias,
    a_log,
    d_skip,
    norm_gain,
    resid,
    w_out,
    final_gain,
    head_weight,
    lengths,
):
    rows = xs.shape[0]
    inner = xs.shape[1]
    seq_count = lax.axis_size("seq")
    place = lax.axis_index("seq")
    heads_all = a_log.shape[0]
    heads = heads_all // seq_count
    groups = NGROUPS // seq_count
    share = inner // seq_count
    bshare = groups * STATE
    group_rows = rows * seq_count

    def by_dest(part, width):
        return part.reshape(rows, seq_count, width).transpose(1, 0, 2)

    packed = jnp.concatenate(
        [
            by_dest(xs, share),
            by_dest(zgate, share),
            by_dest(bc[:, : NGROUPS * STATE], bshare),
            by_dest(bc[:, NGROUPS * STATE :], bshare),
            by_dest(dt_raw, heads),
        ],
        axis=2,
    )
    moved = lax.all_to_all(packed, "seq", split_axis=0, concat_axis=0, tiled=True)
    moved = moved.reshape(group_rows, -1)
    xg = moved[:, :share]
    zg = moved[:, share : 2 * share]
    bg = moved[:, 2 * share : 2 * share + bshare]
    cg = moved[:, 2 * share + bshare : 2 * share + 2 * bshare]
    dg = moved[:, 2 * share + 2 * bshare :]

    my_heads = lambda v: lax.dynamic_slice_in_dim(v, place * heads, heads)
    rate = jnp.exp(my_heads(a_log))
    skipw = my_heads(d_skip)
    steps_dt = jax.nn.softplus(dg.astype(jnp.float32) + my_heads(dt_bias)[None, :])

    lens = lengths[0]
    slots = lens.shape[0]
    ends = jnp.cumsum(lens)
    positions = jnp.arange(group_rows, dtype=jnp.int32)
    segment = jnp.sum((positions[:, None] >= ends[None, :]).astype(jnp.int32), axis=1)
    live = segment < slots

    state_in = jnp.zeros((heads, HEAD_DIM, STATE), jnp.float32)
    prev_seg = jnp.array(-1, jnp.int32)
    ys = []
    for chunk in range(seq_count):
        lo, hi = chunk * rows, (chunk + 1) * rows
        local, keep, state, carry_w, cmat = block_terms(
            xg[lo:hi], bg[lo:hi], cg[lo:hi], steps_dt[lo:hi], segment[lo:hi], live[lo:hi],
            prev_seg, rate, skipw, groups,
        )
        y4 = (local + carry_term(state_in, cmat, carry_w, groups)) * live[lo:hi].astype(
            jnp.float32
        )[:, None, None, None]
        ys.append(y4.reshape(rows, share))
        state_in = keep[:, None, None] * state_in + state
        prev_seg = segment[hi - 1]
    y = jnp.concatenate(ys, axis=0)
    gain = lax.dynamic_slice_in_dim(norm_gain, place * share, share)
    gated = gate_norm(y, zg, gain, groups)

    width = resid.shape[1]
    w_cols = lax.dynamic_slice_in_dim(w_out, place * width, width, axis=1)
    w_full = lax.all_gather(w_cols, "req", axis=0, tiled=True)
    gated_all = lax.all_gather(gated, "seq", axis=1, tiled=True)
    mixer = jnp.dot(gated_all, w_full, preferred_element_type=jnp.float32).astype(jnp.bfloat16)
    layer_out = (resid.astype(jnp.float32) + mixer.astype(jnp.float32)).astype(jnp.bfloat16)

    group_pos = jnp.arange(group_rows, dtype=jnp.int32)
    picker = (group_pos[None, :] == (ends - 1)[:, None]).astype(jnp.bfloat16)
    picked_rows = jnp.dot(picker, layer_out, preferred_element_type=jnp.float32).astype(
        jnp.bfloat16
    )
    row_pair = lax.all_gather(picked_rows, "seq", axis=1, tiled=True)
    collected = lax.all_gather(row_pair, "req", axis=0, tiled=True)
    last_rows = collected.astype(jnp.float32)
    meansq = jnp.mean(last_rows * last_rows, axis=-1, keepdims=True)
    normed = (last_rows * lax.rsqrt(meansq + 1e-05) * final_gain[None, :]).astype(jnp.bfloat16)
    logits = jnp.dot(normed, head_weight, preferred_element_type=jnp.float32)
    return (layer_out, logits)


def solution(mesh):
    placed = (
        P(("req", "seq"), None),
        P(("req", "seq"), None),
        P(("req", "seq"), None),
        P(("req", "seq"), None),
        P(),
        P(),
        P(),
        P(),
        P("req", "seq"),
        P("req", None),
        P(),
        P(None, ("req", "seq")),
        P("req", None),
    )
    return jax.shard_map(
        mixer_layer,
        mesh=mesh,
        in_specs=placed,
        out_specs=(P("req", "seq"), P(None, ("req", "seq"))),
        check_vma=False,
    )
```

```python
import jax
import jax.numpy as jnp
from jax import lax
from jax.sharding import PartitionSpec as P

HEAD_DIM = 64
NGROUPS = 8
STATE = 128


def split_halves(value):
    upper = value.astype(jnp.bfloat16)
    lower = (value - upper.astype(jnp.float32)).astype(jnp.bfloat16)
    return (upper, lower)


def group_inner(operands):
    cum_g, scores_g, inflow_g, x_g, allowed_mask = operands
    diff = cum_g[:, None, :] - cum_g[None, :, :]
    decay = jnp.where(allowed_mask[:, :, None], jnp.exp(jnp.minimum(diff, 0.0)), 0.0)
    weights = decay * scores_g[:, :, None] * inflow_g[None, :, :]
    upper, lower = split_halves(weights)
    first_part = jnp.einsum("tsk,skp->tkp", upper, x_g, preferred_element_type=jnp.float32)
    second_part = jnp.einsum("tsk,skp->tkp", lower, x_g, preferred_element_type=jnp.float32)
    return first_part + second_part


def block_terms(xb, bb, cb, dtb, segment, live, prev_seg, rate, d_skip, groups):
    rows = xb.shape[0]
    heads = rate.shape[0]
    per_group = heads // groups
    x4 = xb.reshape(rows, groups, per_group, HEAD_DIM)
    bmat = bb.reshape(rows, groups, STATE)
    cmat = cb.reshape(rows, groups, STATE)
    livef = live.astype(jnp.float32)
    cum = jnp.cumsum(-rate[None, :] * dtb, axis=0)
    inflow = dtb * livef[:, None]
    index = jnp.arange(rows, dtype=jnp.int32)
    allowed_mask = (segment[:, None] == segment[None, :]) & (index[:, None] >= index[None, :])
    scores = jnp.einsum("tgn,sgn->gts", cmat, bmat, preferred_element_type=jnp.float32)
    cum_g = cum.reshape(rows, groups, per_group).transpose(1, 0, 2)
    inflow_g = inflow.reshape(rows, groups, per_group).transpose(1, 0, 2)
    x_g = x4.transpose(1, 0, 2, 3)
    allowed_all = jnp.broadcast_to(allowed_mask[None], (groups, rows, rows))
    y_groups = lax.map(group_inner, (cum_g, scores, inflow_g, x_g, allowed_all))
    y_inner = y_groups.transpose(1, 0, 2, 3)
    skip = d_skip.reshape(1, groups, per_group, 1) * x4.astype(jnp.float32)
    last_seg = segment[rows - 1]
    tail = (
        jnp.exp(cum[rows - 1][None, :] - cum)
        * (segment == last_seg).astype(jnp.float32)[:, None]
        * inflow
    )
    scaled = tail.reshape(rows, groups, per_group, 1) * x4.astype(jnp.float32)
    upper, lower = split_halves(scaled)
    state = jnp.einsum("sgkp,sgn->gkpn", upper, bmat, preferred_element_type=jnp.float32)
    state = state + jnp.einsum("sgkp,sgn->gkpn", lower, bmat, preferred_element_type=jnp.float32)
    keep = jnp.exp(cum[rows - 1]) * (last_seg == prev_seg).astype(jnp.float32)
    carry_w = jnp.exp(cum) * (segment == prev_seg).astype(jnp.float32)[:, None]
    return (y_inner + skip, keep, state.reshape(heads, HEAD_DIM, STATE), carry_w, cmat)


def carry_term(arriving_vector, cmat, carry_w, groups):
    rows = cmat.shape[0]
    heads = arriving_vector.shape[0]
    per_group = heads // groups
    state4 = arriving_vector.reshape(groups, per_group, HEAD_DIM, STATE)
    upper, lower = split_halves(state4)
    y_carry = jnp.einsum("tgn,gkpn->tgkp", cmat, upper, preferred_element_type=jnp.float32)
    y_carry = y_carry + jnp.einsum(
        "tgn,gkpn->tgkp", cmat, lower, preferred_element_type=jnp.float32
    )
    return y_carry * carry_w.reshape(rows, groups, per_group, 1)


def gate_norm(y, zgate, norm_gain, groups):
    rows = y.shape[0]
    gated = y * jax.nn.silu(zgate.astype(jnp.float32))
    blocks = gated.reshape(rows, groups, -1)
    meansq = jnp.mean(blocks * blocks, axis=-1, keepdims=True)
    normed = (blocks * lax.rsqrt(meansq + 1e-05)).reshape(rows, -1) * norm_gain[None, :]
    return normed.astype(jnp.bfloat16)


def mixer_layer(
    xs,
    bc,
    zgate,
    dt_raw,
    dt_bias,
    a_log,
    d_skip,
    norm_gain,
    resid,
    w_out,
    final_gain,
    head_weight,
    lengths,
):
    rows = xs.shape[0]
    inner = xs.shape[1]
    seq_count = lax.axis_size("seq")
    place = lax.axis_index("seq")
    heads_all = a_log.shape[0]
    heads = heads_all // seq_count
    groups = NGROUPS // seq_count
    share = inner // seq_count
    bshare = groups * STATE
    group_rows = rows * seq_count

    def by_dest(part, width):
        return part.reshape(rows, seq_count, width).transpose(1, 0, 2)

    def to_heads(part, width):
        moved = lax.all_to_all(by_dest(part, width), "seq", split_axis=0, concat_axis=0, tiled=True)
        return moved.reshape(group_rows, width)

    xg = to_heads(xs, share)
    bg = to_heads(bc[:, : NGROUPS * STATE], bshare)
    cg = to_heads(bc[:, NGROUPS * STATE :], bshare)
    dg = to_heads(dt_raw, heads)
    zg = to_heads(zgate, share)

    my_heads = lambda v: lax.dynamic_slice_in_dim(v, place * heads, heads)
    rate = jnp.exp(my_heads(a_log))
    skipw = my_heads(d_skip)
    steps_dt = jax.nn.softplus(dg.astype(jnp.float32) + my_heads(dt_bias)[None, :])

    lens = lengths[0]
    slots = lens.shape[0]
    ends = jnp.cumsum(lens)
    positions = jnp.arange(group_rows, dtype=jnp.int32)
    segment = jnp.sum((positions[:, None] >= ends[None, :]).astype(jnp.int32), axis=1)
    live = segment < slots

    gain = lax.dynamic_slice_in_dim(norm_gain, place * share, share)
    width = resid.shape[1]
    w_cols = lax.dynamic_slice_in_dim(w_out, place * width, width, axis=1)
    w_full = lax.all_gather(w_cols, "req", axis=0, tiled=True)

    state_in = jnp.zeros((heads, HEAD_DIM, STATE), jnp.float32)
    prev_seg = jnp.array(-1, jnp.int32)
    inputs = (xg, bg, cg, steps_dt)
    mixers = []
    for chunk in range(seq_count):
        lo, hi = chunk * rows, (chunk + 1) * rows
        xb, bb, cb, db = (part[lo:hi] for part in inputs)
        if chunk > 0:
            xb, bb, cb, db = lax.optimization_barrier((xb, bb, cb, db, gated))[:4]
        local, keep, state, carry_w, cmat = block_terms(
            xb, bb, cb, db, segment[lo:hi], live[lo:hi], prev_seg, rate, skipw, groups,
        )
        y4 = (local + carry_term(state_in, cmat, carry_w, groups)) * live[lo:hi].astype(
            jnp.float32
        )[:, None, None, None]
        state_in = keep[:, None, None] * state_in + state
        prev_seg = segment[hi - 1]
        gated = gate_norm(y4.reshape(rows, share), zg[lo:hi], gain, groups)
        gated_all = lax.all_gather(gated, "seq", axis=1, tiled=True)
        mixers.append(jnp.dot(gated_all, w_full, preferred_element_type=jnp.float32))
    mixer = jnp.concatenate(mixers, axis=0).astype(jnp.bfloat16)
    layer_out = (resid.astype(jnp.float32) + mixer.astype(jnp.float32)).astype(jnp.bfloat16)

    group_pos = jnp.arange(group_rows, dtype=jnp.int32)
    picker = (group_pos[None, :] == (ends - 1)[:, None]).astype(jnp.bfloat16)
    picked_rows = jnp.dot(picker, layer_out, preferred_element_type=jnp.float32).astype(
        jnp.bfloat16
    )
    row_pair = lax.all_gather(picked_rows, "seq", axis=1, tiled=True)
    collected = lax.all_gather(row_pair, "req", axis=0, tiled=True)
    last_rows = collected.astype(jnp.float32)
    meansq = jnp.mean(last_rows * last_rows, axis=-1, keepdims=True)
    normed = (last_rows * lax.rsqrt(meansq + 1e-05) * final_gain[None, :]).astype(jnp.bfloat16)
    logits = jnp.dot(normed, head_weight, preferred_element_type=jnp.float32)
    return (layer_out, logits)


def solution(mesh):
    placed = (
        P(("req", "seq"), None),
        P(("req", "seq"), None),
        P(("req", "seq"), None),
        P(("req", "seq"), None),
        P(),
        P(),
        P(),
        P(),
        P("req", "seq"),
        P("req", None),
        P(),
        P(None, ("req", "seq")),
        P("req", None),
    )
    return jax.shard_map(
        mixer_layer,
        mesh=mesh,
        in_specs=placed,
        out_specs=(P("req", "seq"), P(None, ("req", "seq"))),
        check_vma=False,
    )
```

```python
import jax
import jax.numpy as jnp
from jax import lax
from jax.sharding import PartitionSpec as P

HEAD_DIM = 64
NGROUPS = 8
STATE = 128


def split_halves(value):
    upper = value.astype(jnp.bfloat16)
    lower = (value - upper.astype(jnp.float32)).astype(jnp.bfloat16)
    return (upper, lower)


def group_inner(operands):
    cum_g, scores_g, inflow_g, x_g, allowed_mask = operands
    diff = cum_g[:, None, :] - cum_g[None, :, :]
    decay = jnp.where(allowed_mask[:, :, None], jnp.exp(jnp.minimum(diff, 0.0)), 0.0)
    weights = decay * scores_g[:, :, None] * inflow_g[None, :, :]
    upper, lower = split_halves(weights)
    first_part = jnp.einsum("tsk,skp->tkp", upper, x_g, preferred_element_type=jnp.float32)
    second_part = jnp.einsum("tsk,skp->tkp", lower, x_g, preferred_element_type=jnp.float32)
    return first_part + second_part


def block_terms(xb, bb, cb, dtb, segment, live, prev_seg, rate, d_skip, groups):
    rows = xb.shape[0]
    heads = rate.shape[0]
    per_group = heads // groups
    x4 = xb.reshape(rows, groups, per_group, HEAD_DIM)
    bmat = bb.reshape(rows, groups, STATE)
    cmat = cb.reshape(rows, groups, STATE)
    livef = live.astype(jnp.float32)
    cum = jnp.cumsum(-rate[None, :] * dtb, axis=0)
    inflow = dtb * livef[:, None]
    index = jnp.arange(rows, dtype=jnp.int32)
    allowed_mask = (segment[:, None] == segment[None, :]) & (index[:, None] >= index[None, :])
    scores = jnp.einsum("tgn,sgn->gts", cmat, bmat, preferred_element_type=jnp.float32)
    cum_g = cum.reshape(rows, groups, per_group).transpose(1, 0, 2)
    inflow_g = inflow.reshape(rows, groups, per_group).transpose(1, 0, 2)
    x_g = x4.transpose(1, 0, 2, 3)
    allowed_all = jnp.broadcast_to(allowed_mask[None], (groups, rows, rows))
    y_groups = lax.map(group_inner, (cum_g, scores, inflow_g, x_g, allowed_all))
    y_inner = y_groups.transpose(1, 0, 2, 3)
    skip = d_skip.reshape(1, groups, per_group, 1) * x4.astype(jnp.float32)
    last_seg = segment[rows - 1]
    tail = (
        jnp.exp(cum[rows - 1][None, :] - cum)
        * (segment == last_seg).astype(jnp.float32)[:, None]
        * inflow
    )
    scaled = tail.reshape(rows, groups, per_group, 1) * x4.astype(jnp.float32)
    upper, lower = split_halves(scaled)
    state = jnp.einsum("sgkp,sgn->gkpn", upper, bmat, preferred_element_type=jnp.float32)
    state = state + jnp.einsum("sgkp,sgn->gkpn", lower, bmat, preferred_element_type=jnp.float32)
    keep = jnp.exp(cum[rows - 1]) * (last_seg == prev_seg).astype(jnp.float32)
    carry_w = jnp.exp(cum) * (segment == prev_seg).astype(jnp.float32)[:, None]
    return (y_inner + skip, keep, state.reshape(heads, HEAD_DIM, STATE), carry_w, cmat)


def carry_term(arriving_vector, cmat, carry_w, groups):
    rows = cmat.shape[0]
    heads = arriving_vector.shape[0]
    per_group = heads // groups
    state4 = arriving_vector.reshape(groups, per_group, HEAD_DIM, STATE)
    upper, lower = split_halves(state4)
    y_carry = jnp.einsum("tgn,gkpn->tgkp", cmat, upper, preferred_element_type=jnp.float32)
    y_carry = y_carry + jnp.einsum(
        "tgn,gkpn->tgkp", cmat, lower, preferred_element_type=jnp.float32
    )
    return y_carry * carry_w.reshape(rows, groups, per_group, 1)


def gate_norm(y, zgate, norm_gain, groups):
    rows = y.shape[0]
    gated = y * jax.nn.silu(zgate.astype(jnp.float32))
    blocks = gated.reshape(rows, groups, -1)
    meansq = jnp.mean(blocks * blocks, axis=-1, keepdims=True)
    normed = (blocks * lax.rsqrt(meansq + 1e-05)).reshape(rows, -1) * norm_gain[None, :]
    return normed.astype(jnp.bfloat16)


def mixer_layer(
    xs,
    bc,
    zgate,
    dt_raw,
    dt_bias,
    a_log,
    d_skip,
    norm_gain,
    resid,
    w_out,
    final_gain,
    head_weight,
    lengths,
):
    rows = xs.shape[0]
    inner = xs.shape[1]
    seq_count = lax.axis_size("seq")
    place = lax.axis_index("seq")
    heads_all = a_log.shape[0]
    heads = heads_all // seq_count
    groups = NGROUPS // seq_count
    share = inner // seq_count
    bshare = groups * STATE
    group_rows = rows * seq_count

    def by_dest(part, width):
        return part.reshape(rows, seq_count, width).transpose(1, 0, 2)

    packed = jnp.concatenate(
        [
            by_dest(xs, share),
            by_dest(zgate, share),
            by_dest(bc[:, : NGROUPS * STATE], bshare),
            by_dest(bc[:, NGROUPS * STATE :], bshare),
            by_dest(dt_raw, heads),
        ],
        axis=2,
    )
    moved = lax.all_to_all(packed, "seq", split_axis=0, concat_axis=0, tiled=True)
    moved = moved.reshape(group_rows, -1)
    xg = moved[:, :share]
    zg = moved[:, share : 2 * share]
    bg = moved[:, 2 * share : 2 * share + bshare]
    cg = moved[:, 2 * share + bshare : 2 * share + 2 * bshare]
    dg = moved[:, 2 * share + 2 * bshare :]

    my_heads = lambda v: lax.dynamic_slice_in_dim(v, place * heads, heads)
    rate = jnp.exp(my_heads(a_log))
    skipw = my_heads(d_skip)
    steps_dt = jax.nn.softplus(dg.astype(jnp.float32) + my_heads(dt_bias)[None, :])

    lens = lengths[0]
    slots = lens.shape[0]
    ends = jnp.cumsum(lens)
    positions = jnp.arange(group_rows, dtype=jnp.int32)
    segment = jnp.sum((positions[:, None] >= ends[None, :]).astype(jnp.int32), axis=1)
    live = segment < slots

    state_in = jnp.zeros((heads, HEAD_DIM, STATE), jnp.float32)
    prev_seg = jnp.array(-1, jnp.int32)
    ys = []
    for chunk in range(seq_count):
        lo, hi = chunk * rows, (chunk + 1) * rows
        local, keep, state, carry_w, cmat = block_terms(
            xg[lo:hi], bg[lo:hi], cg[lo:hi], steps_dt[lo:hi], segment[lo:hi], live[lo:hi],
            prev_seg, rate, skipw, groups,
        )
        y4 = (local + carry_term(state_in, cmat, carry_w, groups)) * live[lo:hi].astype(
            jnp.float32
        )[:, None, None, None]
        ys.append(y4.reshape(rows, share))
        state_in = keep[:, None, None] * state_in + state
        prev_seg = segment[hi - 1]
    y = jnp.concatenate(ys, axis=0)
    gain = lax.dynamic_slice_in_dim(norm_gain, place * share, share)
    gated = gate_norm(y, zg, gain, groups)

    width = resid.shape[1]
    w_cols = lax.dynamic_slice_in_dim(w_out, place * width, width, axis=1)
    w_full = lax.all_gather(w_cols, "req", axis=0, tiled=True)
    gated_all = lax.all_gather(gated, "seq", axis=1, tiled=True)
    mixer = jnp.dot(gated_all, w_full, preferred_element_type=jnp.float32).astype(jnp.bfloat16)
    layer_out = (resid.astype(jnp.float32) + mixer.astype(jnp.float32)).astype(jnp.bfloat16)

    group_pos = jnp.arange(group_rows, dtype=jnp.int32)
    picker = (group_pos[None, :] == (ends - 1)[:, None]).astype(jnp.bfloat16)
    picked_gated = jnp.dot(picker, gated_all, preferred_element_type=jnp.float32).astype(jnp.bfloat16)
    picked_resid = jnp.dot(picker, resid, preferred_element_type=jnp.float32)
    picked_mixer = jnp.dot(picked_gated, w_full, preferred_element_type=jnp.float32)
    picked_rows = (picked_resid + picked_mixer.astype(jnp.bfloat16).astype(jnp.float32)).astype(
        jnp.bfloat16
    )
    owner = lax.axis_index("req")
    owners_all = lax.axis_size("req")
    spread = jnp.zeros((owners_all, slots, seq_count, width), jnp.bfloat16)
    spread = lax.dynamic_update_slice(spread, picked_rows[None, :, None, :], (owner, 0, place, 0))
    collected = lax.psum(spread, ("req", "seq"))
    last_rows = collected.reshape(owners_all * slots, seq_count * width).astype(jnp.float32)
    meansq = jnp.mean(last_rows * last_rows, axis=-1, keepdims=True)
    normed = (last_rows * lax.rsqrt(meansq + 1e-05) * final_gain[None, :]).astype(jnp.bfloat16)
    logits = jnp.dot(normed, head_weight, preferred_element_type=jnp.float32)
    return (layer_out, logits)


def solution(mesh):
    placed = (
        P(("req", "seq"), None),
        P(("req", "seq"), None),
        P(("req", "seq"), None),
        P(("req", "seq"), None),
        P(),
        P(),
        P(),
        P(),
        P("req", "seq"),
        P("req", None),
        P(),
        P(None, ("req", "seq")),
        P("req", None),
    )
    return jax.shard_map(
        mixer_layer,
        mesh=mesh,
        in_specs=placed,
        out_specs=(P("req", "seq"), P(None, ("req", "seq"))),
        check_vma=False,
    )
```

```python
import jax
import jax.numpy as jnp
from jax import lax
from jax.sharding import PartitionSpec as P

HEAD_DIM = 64
NGROUPS = 8
STATE = 128


def split_halves(value):
    upper = value.astype(jnp.bfloat16)
    lower = (value - upper.astype(jnp.float32)).astype(jnp.bfloat16)
    return (upper, lower)


def group_inner(operands):
    cum_g, scores_g, inflow_g, x_g, allowed_mask = operands
    diff = cum_g[:, None, :] - cum_g[None, :, :]
    decay = jnp.where(allowed_mask[:, :, None], jnp.exp(jnp.minimum(diff, 0.0)), 0.0)
    weights = decay * scores_g[:, :, None] * inflow_g[None, :, :]
    upper, lower = split_halves(weights)
    first_part = jnp.einsum("tsk,skp->tkp", upper, x_g, preferred_element_type=jnp.float32)
    second_part = jnp.einsum("tsk,skp->tkp", lower, x_g, preferred_element_type=jnp.float32)
    return first_part + second_part


def block_terms(xb, bb, cb, dtb, segment, live, prev_seg, rate, d_skip, groups):
    rows = xb.shape[0]
    heads = rate.shape[0]
    per_group = heads // groups
    x4 = xb.reshape(rows, groups, per_group, HEAD_DIM)
    bmat = bb.reshape(rows, groups, STATE)
    cmat = cb.reshape(rows, groups, STATE)
    livef = live.astype(jnp.float32)
    cum = jnp.cumsum(-rate[None, :] * dtb, axis=0)
    inflow = dtb * livef[:, None]
    index = jnp.arange(rows, dtype=jnp.int32)
    allowed_mask = (segment[:, None] == segment[None, :]) & (index[:, None] >= index[None, :])
    scores = jnp.einsum("tgn,sgn->gts", cmat, bmat, preferred_element_type=jnp.float32)
    cum_g = cum.reshape(rows, groups, per_group).transpose(1, 0, 2)
    inflow_g = inflow.reshape(rows, groups, per_group).transpose(1, 0, 2)
    x_g = x4.transpose(1, 0, 2, 3)
    allowed_all = jnp.broadcast_to(allowed_mask[None], (groups, rows, rows))
    y_groups = lax.map(group_inner, (cum_g, scores, inflow_g, x_g, allowed_all))
    y_inner = y_groups.transpose(1, 0, 2, 3)
    skip = d_skip.reshape(1, groups, per_group, 1) * x4.astype(jnp.float32)
    last_seg = segment[rows - 1]
    tail = (
        jnp.exp(cum[rows - 1][None, :] - cum)
        * (segment == last_seg).astype(jnp.float32)[:, None]
        * inflow
    )
    scaled = tail.reshape(rows, groups, per_group, 1) * x4.astype(jnp.float32)
    upper, lower = split_halves(scaled)
    state = jnp.einsum("sgkp,sgn->gkpn", upper, bmat, preferred_element_type=jnp.float32)
    state = state + jnp.einsum("sgkp,sgn->gkpn", lower, bmat, preferred_element_type=jnp.float32)
    keep = jnp.exp(cum[rows - 1]) * (last_seg == prev_seg).astype(jnp.float32)
    carry_w = jnp.exp(cum) * (segment == prev_seg).astype(jnp.float32)[:, None]
    return (y_inner + skip, keep, state.reshape(heads, HEAD_DIM, STATE), carry_w, cmat)


def carry_term(arriving_vector, cmat, carry_w, groups):
    rows = cmat.shape[0]
    heads = arriving_vector.shape[0]
    per_group = heads // groups
    state4 = arriving_vector.reshape(groups, per_group, HEAD_DIM, STATE)
    upper, lower = split_halves(state4)
    y_carry = jnp.einsum("tgn,gkpn->tgkp", cmat, upper, preferred_element_type=jnp.float32)
    y_carry = y_carry + jnp.einsum(
        "tgn,gkpn->tgkp", cmat, lower, preferred_element_type=jnp.float32
    )
    return y_carry * carry_w.reshape(rows, groups, per_group, 1)


def gate_norm(y, zgate, norm_gain, groups):
    rows = y.shape[0]
    gated = y * jax.nn.silu(zgate.astype(jnp.float32))
    blocks = gated.reshape(rows, groups, -1)
    meansq = jnp.mean(blocks * blocks, axis=-1, keepdims=True)
    normed = (blocks * lax.rsqrt(meansq + 1e-05)).reshape(rows, -1) * norm_gain[None, :]
    return normed.astype(jnp.bfloat16)


def mixer_layer(
    xs,
    bc,
    zgate,
    dt_raw,
    dt_bias,
    a_log,
    d_skip,
    norm_gain,
    resid,
    w_out,
    final_gain,
    head_weight,
    lengths,
):
    rows = xs.shape[0]
    inner = xs.shape[1]
    seq_count = lax.axis_size("seq")
    place = lax.axis_index("seq")
    heads_all = a_log.shape[0]
    heads = heads_all // seq_count
    groups = NGROUPS // seq_count
    share = inner // seq_count
    bshare = groups * STATE
    group_rows = rows * seq_count

    def by_dest(part, width):
        return part.reshape(rows, seq_count, width).transpose(1, 0, 2)

    packed = jnp.concatenate(
        [
            by_dest(xs, share),
            by_dest(zgate, share),
            by_dest(bc[:, : NGROUPS * STATE], bshare),
            by_dest(bc[:, NGROUPS * STATE :], bshare),
            by_dest(dt_raw, heads),
        ],
        axis=2,
    )
    moved = lax.all_to_all(packed, "seq", split_axis=0, concat_axis=0, tiled=True)
    moved = moved.reshape(group_rows, -1)
    xg = moved[:, :share]
    zg = moved[:, share : 2 * share]
    bg = moved[:, 2 * share : 2 * share + bshare]
    cg = moved[:, 2 * share + bshare : 2 * share + 2 * bshare]
    dg = moved[:, 2 * share + 2 * bshare :]

    my_heads = lambda v: lax.dynamic_slice_in_dim(v, place * heads, heads)
    rate = jnp.exp(my_heads(a_log))
    skipw = my_heads(d_skip)
    steps_dt = jax.nn.softplus(dg.astype(jnp.float32) + my_heads(dt_bias)[None, :])

    lens = lengths[0]
    slots = lens.shape[0]
    ends = jnp.cumsum(lens)
    positions = jnp.arange(group_rows, dtype=jnp.int32)
    segment = jnp.sum((positions[:, None] >= ends[None, :]).astype(jnp.int32), axis=1)
    live = segment < slots

    state_in = jnp.zeros((heads, HEAD_DIM, STATE), jnp.float32)
    prev_seg = jnp.array(-1, jnp.int32)
    ys = []
    for chunk in range(seq_count):
        lo, hi = chunk * rows, (chunk + 1) * rows
        local, keep, state, carry_w, cmat = block_terms(
            xg[lo:hi], bg[lo:hi], cg[lo:hi], steps_dt[lo:hi], segment[lo:hi], live[lo:hi],
            prev_seg, rate, skipw, groups,
        )
        y4 = (local + carry_term(state_in, cmat, carry_w, groups)) * live[lo:hi].astype(
            jnp.float32
        )[:, None, None, None]
        ys.append(y4.reshape(rows, share))
        state_in = keep[:, None, None] * state_in + state
        prev_seg = segment[hi - 1]
    y = jnp.concatenate(ys, axis=0)
    gain = lax.dynamic_slice_in_dim(norm_gain, place * share, share)
    gated = gate_norm(y, zg, gain, groups)

    width = resid.shape[1]
    w_cols = lax.dynamic_slice_in_dim(w_out, place * width, width, axis=1)
    w_full = lax.all_gather(w_cols, "req", axis=0, tiled=True)
    gated_all = lax.all_gather(gated, "seq", axis=1, tiled=True)

    group_pos = jnp.arange(group_rows, dtype=jnp.int32)
    picker = (group_pos[None, :] == (ends - 1)[:, None]).astype(jnp.bfloat16)
    picked_gated = jnp.dot(picker, gated, preferred_element_type=jnp.float32).astype(jnp.bfloat16)
    picked_gated = lax.all_gather(picked_gated, "seq", axis=1, tiled=True)
    picked_resid = jnp.dot(picker, resid, preferred_element_type=jnp.float32)
    picked_mixer = jnp.dot(picked_gated, w_full, preferred_element_type=jnp.float32)
    picked_rows = (
        picked_resid + picked_mixer.astype(jnp.bfloat16).astype(jnp.float32)
    ).astype(jnp.bfloat16)
    row_pair = lax.all_gather(picked_rows, "seq", axis=1, tiled=True)
    collected = lax.all_gather(row_pair, "req", axis=0, tiled=True)
    last_rows = collected.astype(jnp.float32)
    meansq = jnp.mean(last_rows * last_rows, axis=-1, keepdims=True)
    normed = (last_rows * lax.rsqrt(meansq + 1e-05) * final_gain[None, :]).astype(jnp.bfloat16)
    logits = jnp.dot(normed, head_weight, preferred_element_type=jnp.float32)

    mixer = jnp.dot(gated_all, w_full, preferred_element_type=jnp.float32).astype(jnp.bfloat16)
    layer_out = (resid.astype(jnp.float32) + mixer.astype(jnp.float32)).astype(jnp.bfloat16)
    return (layer_out, logits)


def solution(mesh):
    placed = (
        P(("req", "seq"), None),
        P(("req", "seq"), None),
        P(("req", "seq"), None),
        P(("req", "seq"), None),
        P(),
        P(),
        P(),
        P(),
        P("req", "seq"),
        P("req", None),
        P(),
        P(None, ("req", "seq")),
        P("req", None),
    )
    return jax.shard_map(
        mixer_layer,
        mesh=mesh,
        in_specs=placed,
        out_specs=(P("req", "seq"), P(None, ("req", "seq"))),
        check_vma=False,
    )
```

```python
import jax
import jax.numpy as jnp
from jax import lax
from jax.sharding import PartitionSpec as P

HEAD_DIM = 64
NGROUPS = 8
STATE = 128


def split_halves(value):
    upper = value.astype(jnp.bfloat16)
    lower = (value - upper.astype(jnp.float32)).astype(jnp.bfloat16)
    return (upper, lower)


def group_inner(operands):
    cum_g, scores_g, inflow_g, x_g, allowed_mask = operands
    diff = cum_g[:, None, :] - cum_g[None, :, :]
    decay = jnp.where(allowed_mask[:, :, None], jnp.exp(jnp.minimum(diff, 0.0)), 0.0)
    weights = decay * scores_g[:, :, None] * inflow_g[None, :, :]
    upper, lower = split_halves(weights)
    first_part = jnp.einsum("tsk,skp->tkp", upper, x_g, preferred_element_type=jnp.float32)
    second_part = jnp.einsum("tsk,skp->tkp", lower, x_g, preferred_element_type=jnp.float32)
    return first_part + second_part


def block_terms(xb, bb, cb, dtb, segment, live, prev_seg, rate, d_skip, groups):
    rows = xb.shape[0]
    heads = rate.shape[0]
    per_group = heads // groups
    x4 = xb.reshape(rows, groups, per_group, HEAD_DIM)
    bmat = bb.reshape(rows, groups, STATE)
    cmat = cb.reshape(rows, groups, STATE)
    livef = live.astype(jnp.float32)
    cum = jnp.cumsum(-rate[None, :] * dtb, axis=0)
    inflow = dtb * livef[:, None]
    index = jnp.arange(rows, dtype=jnp.int32)
    allowed_mask = (segment[:, None] == segment[None, :]) & (index[:, None] >= index[None, :])
    scores = jnp.einsum("tgn,sgn->gts", cmat, bmat, preferred_element_type=jnp.float32)
    cum_g = cum.reshape(rows, groups, per_group).transpose(1, 0, 2)
    inflow_g = inflow.reshape(rows, groups, per_group).transpose(1, 0, 2)
    x_g = x4.transpose(1, 0, 2, 3)
    allowed_all = jnp.broadcast_to(allowed_mask[None], (groups, rows, rows))
    y_groups = lax.map(group_inner, (cum_g, scores, inflow_g, x_g, allowed_all))
    y_inner = y_groups.transpose(1, 0, 2, 3)
    skip = d_skip.reshape(1, groups, per_group, 1) * x4.astype(jnp.float32)
    last_seg = segment[rows - 1]
    tail = (
        jnp.exp(cum[rows - 1][None, :] - cum)
        * (segment == last_seg).astype(jnp.float32)[:, None]
        * inflow
    )
    scaled = tail.reshape(rows, groups, per_group, 1) * x4.astype(jnp.float32)
    upper, lower = split_halves(scaled)
    state = jnp.einsum("sgkp,sgn->gkpn", upper, bmat, preferred_element_type=jnp.float32)
    state = state + jnp.einsum("sgkp,sgn->gkpn", lower, bmat, preferred_element_type=jnp.float32)
    keep = jnp.exp(cum[rows - 1]) * (last_seg == prev_seg).astype(jnp.float32)
    carry_w = jnp.exp(cum) * (segment == prev_seg).astype(jnp.float32)[:, None]
    return (y_inner + skip, keep, state.reshape(heads, HEAD_DIM, STATE), carry_w, cmat)


def carry_term(arriving_vector, cmat, carry_w, groups):
    rows = cmat.shape[0]
    heads = arriving_vector.shape[0]
    per_group = heads // groups
    state4 = arriving_vector.reshape(groups, per_group, HEAD_DIM, STATE)
    upper, lower = split_halves(state4)
    y_carry = jnp.einsum("tgn,gkpn->tgkp", cmat, upper, preferred_element_type=jnp.float32)
    y_carry = y_carry + jnp.einsum(
        "tgn,gkpn->tgkp", cmat, lower, preferred_element_type=jnp.float32
    )
    return y_carry * carry_w.reshape(rows, groups, per_group, 1)


def gate_norm(y, zgate, norm_gain, groups):
    rows = y.shape[0]
    gated = y * jax.nn.silu(zgate.astype(jnp.float32))
    blocks = gated.reshape(rows, groups, -1)
    meansq = jnp.mean(blocks * blocks, axis=-1, keepdims=True)
    normed = (blocks * lax.rsqrt(meansq + 1e-05)).reshape(rows, -1) * norm_gain[None, :]
    return normed.astype(jnp.bfloat16)


def mixer_layer(
    xs,
    bc,
    zgate,
    dt_raw,
    dt_bias,
    a_log,
    d_skip,
    norm_gain,
    resid,
    w_out,
    final_gain,
    head_weight,
    lengths,
):
    rows = xs.shape[0]
    inner = xs.shape[1]
    seq_count = lax.axis_size("seq")
    place = lax.axis_index("seq")
    heads_all = a_log.shape[0]
    heads = heads_all // seq_count
    groups = NGROUPS // seq_count
    group_rows = rows * seq_count

    lens = lengths[0]
    slots = lens.shape[0]
    ends = jnp.cumsum(lens)
    positions = jnp.arange(group_rows, dtype=jnp.int32)
    segment = jnp.sum((positions[:, None] >= ends[None, :]).astype(jnp.int32), axis=1)
    live = segment < slots
    group_pos = jnp.arange(group_rows, dtype=jnp.int32)
    picker = (group_pos[None, :] == (ends - 1)[:, None]).astype(jnp.bfloat16)

    width = resid.shape[1]
    w_cols = lax.dynamic_slice_in_dim(w_out, place * width, width, axis=1)
    w_full = lax.all_gather(w_cols, "req", axis=0, tiled=True)
    w_blocks = w_full.reshape(seq_count, groups, inner // NGROUPS, width)

    block_cols = inner // NGROUPS
    block_heads = heads // groups

    def by_dest(part, width_of, half):
        piece = part.reshape(rows, seq_count, groups, width_of)[:, :, half, :]
        return piece.transpose(1, 0, 2)

    moves = []
    for half in range(groups):
        packed = jnp.concatenate(
            [
                by_dest(xs, block_cols, half),
                by_dest(zgate, block_cols, half),
                by_dest(bc[:, : NGROUPS * STATE], STATE, half),
                by_dest(bc[:, NGROUPS * STATE :], STATE, half),
                by_dest(dt_raw, block_heads, half),
            ],
            axis=2,
        )
        moves.append(lax.all_to_all(packed, "seq", split_axis=0, concat_axis=0, tiled=True))

    gated_parts = []
    picked_parts = []
    for half in range(groups):
        moved = moves[half]
        if half > 0:
            moved = lax.optimization_barrier((moved, gated))[0]
        moved = moved.reshape(group_rows, -1)
        xg = moved[:, :block_cols]
        zg = moved[:, block_cols : 2 * block_cols]
        bg = moved[:, 2 * block_cols : 2 * block_cols + STATE]
        cg = moved[:, 2 * block_cols + STATE : 2 * block_cols + 2 * STATE]
        dg = moved[:, 2 * block_cols + 2 * STATE :]

        first_head = (place * groups + half) * block_heads
        my_heads = lambda v: lax.dynamic_slice_in_dim(v, first_head, block_heads)
        rate = jnp.exp(my_heads(a_log))
        skipw = my_heads(d_skip)
        steps_dt = jax.nn.softplus(dg.astype(jnp.float32) + my_heads(dt_bias)[None, :])

        state_in = jnp.zeros((block_heads, HEAD_DIM, STATE), jnp.float32)
        prev_seg = jnp.array(-1, jnp.int32)
        ys = []
        for chunk in range(seq_count):
            lo, hi = chunk * rows, (chunk + 1) * rows
            local, keep, state, carry_w, cmat = block_terms(
                xg[lo:hi], bg[lo:hi], cg[lo:hi], steps_dt[lo:hi], segment[lo:hi], live[lo:hi],
                prev_seg, rate, skipw, 1,
            )
            y4 = (local + carry_term(state_in, cmat, carry_w, 1)) * live[lo:hi].astype(
                jnp.float32
            )[:, None, None, None]
            ys.append(y4.reshape(rows, block_cols))
            state_in = keep[:, None, None] * state_in + state
            prev_seg = segment[hi - 1]
        y = jnp.concatenate(ys, axis=0)
        gain = lax.dynamic_slice_in_dim(norm_gain, (place * groups + half) * block_cols, block_cols)
        gated = gate_norm(y, zg, gain, 1)
        gated_parts.append(lax.all_gather(gated, "seq", axis=1, tiled=True))
        picked = jnp.dot(picker, gated, preferred_element_type=jnp.float32).astype(jnp.bfloat16)
        picked_parts.append(lax.all_gather(picked, "seq", axis=1, tiled=True))

    picked_resid = jnp.dot(picker, resid, preferred_element_type=jnp.float32)
    picked_mixer = sum(
        jnp.dot(picked_parts[half], w_blocks[:, half].reshape(-1, width),
                preferred_element_type=jnp.float32)
        for half in range(groups)
    )
    picked_rows = (
        picked_resid + picked_mixer.astype(jnp.bfloat16).astype(jnp.float32)
    ).astype(jnp.bfloat16)
    row_pair = lax.all_gather(picked_rows, "seq", axis=1, tiled=True)
    collected = lax.all_gather(row_pair, "req", axis=0, tiled=True)
    last_rows = collected.astype(jnp.float32)
    meansq = jnp.mean(last_rows * last_rows, axis=-1, keepdims=True)
    normed = (last_rows * lax.rsqrt(meansq + 1e-05) * final_gain[None, :]).astype(jnp.bfloat16)
    logits = jnp.dot(normed, head_weight, preferred_element_type=jnp.float32)

    mixer_f32 = None
    for half in range(groups):
        part = jnp.dot(gated_parts[half], w_blocks[:, half].reshape(-1, width),
                       preferred_element_type=jnp.float32)
        mixer_f32 = part if mixer_f32 is None else mixer_f32 + part
    mixer = mixer_f32.astype(jnp.bfloat16)
    layer_out = (resid.astype(jnp.float32) + mixer.astype(jnp.float32)).astype(jnp.bfloat16)
    return (layer_out, logits)


def solution(mesh):
    placed = (
        P(("req", "seq"), None),
        P(("req", "seq"), None),
        P(("req", "seq"), None),
        P(("req", "seq"), None),
        P(),
        P(),
        P(),
        P(),
        P("req", "seq"),
        P("req", None),
        P(),
        P(None, ("req", "seq")),
        P("req", None),
    )
    return jax.shard_map(
        mixer_layer,
        mesh=mesh,
        in_specs=placed,
        out_specs=(P("req", "seq"), P(None, ("req", "seq"))),
        check_vma=False,
    )
```

```python
import jax
import jax.numpy as jnp
from jax import lax
from jax.sharding import PartitionSpec as P

HEAD_DIM = 64
NGROUPS = 8
STATE = 128


def split_halves(value):
    upper = value.astype(jnp.bfloat16)
    lower = (value - upper.astype(jnp.float32)).astype(jnp.bfloat16)
    return (upper, lower)


def group_inner(operands):
    cum_g, scores_g, inflow_g, x_g, allowed_mask = operands
    diff = cum_g[:, None, :] - cum_g[None, :, :]
    decay = jnp.where(allowed_mask[:, :, None], jnp.exp(jnp.minimum(diff, 0.0)), 0.0)
    weights = decay * scores_g[:, :, None] * inflow_g[None, :, :]
    upper, lower = split_halves(weights)
    first_part = jnp.einsum("tsk,skp->tkp", upper, x_g, preferred_element_type=jnp.float32)
    second_part = jnp.einsum("tsk,skp->tkp", lower, x_g, preferred_element_type=jnp.float32)
    return first_part + second_part


def block_terms(xb, bb, cb, dtb, segment, live, prev_seg, rate, d_skip, groups):
    rows = xb.shape[0]
    heads = rate.shape[0]
    per_group = heads // groups
    x4 = xb.reshape(rows, groups, per_group, HEAD_DIM)
    bmat = bb.reshape(rows, groups, STATE)
    cmat = cb.reshape(rows, groups, STATE)
    livef = live.astype(jnp.float32)
    cum = jnp.cumsum(-rate[None, :] * dtb, axis=0)
    inflow = dtb * livef[:, None]
    index = jnp.arange(rows, dtype=jnp.int32)
    allowed_mask = (segment[:, None] == segment[None, :]) & (index[:, None] >= index[None, :])
    scores = jnp.einsum("tgn,sgn->gts", cmat, bmat, preferred_element_type=jnp.float32)
    cum_g = cum.reshape(rows, groups, per_group).transpose(1, 0, 2)
    inflow_g = inflow.reshape(rows, groups, per_group).transpose(1, 0, 2)
    x_g = x4.transpose(1, 0, 2, 3)
    allowed_all = jnp.broadcast_to(allowed_mask[None], (groups, rows, rows))
    y_groups = lax.map(group_inner, (cum_g, scores, inflow_g, x_g, allowed_all))
    y_inner = y_groups.transpose(1, 0, 2, 3)
    skip = d_skip.reshape(1, groups, per_group, 1) * x4.astype(jnp.float32)
    last_seg = segment[rows - 1]
    tail = (
        jnp.exp(cum[rows - 1][None, :] - cum)
        * (segment == last_seg).astype(jnp.float32)[:, None]
        * inflow
    )
    scaled = tail.reshape(rows, groups, per_group, 1) * x4.astype(jnp.float32)
    upper, lower = split_halves(scaled)
    state = jnp.einsum("sgkp,sgn->gkpn", upper, bmat, preferred_element_type=jnp.float32)
    state = state + jnp.einsum("sgkp,sgn->gkpn", lower, bmat, preferred_element_type=jnp.float32)
    keep = jnp.exp(cum[rows - 1]) * (last_seg == prev_seg).astype(jnp.float32)
    carry_w = jnp.exp(cum) * (segment == prev_seg).astype(jnp.float32)[:, None]
    return (y_inner + skip, keep, state.reshape(heads, HEAD_DIM, STATE), carry_w, cmat)


def carry_term(arriving_vector, cmat, carry_w, groups):
    rows = cmat.shape[0]
    heads = arriving_vector.shape[0]
    per_group = heads // groups
    state4 = arriving_vector.reshape(groups, per_group, HEAD_DIM, STATE)
    upper, lower = split_halves(state4)
    y_carry = jnp.einsum("tgn,gkpn->tgkp", cmat, upper, preferred_element_type=jnp.float32)
    y_carry = y_carry + jnp.einsum(
        "tgn,gkpn->tgkp", cmat, lower, preferred_element_type=jnp.float32
    )
    return y_carry * carry_w.reshape(rows, groups, per_group, 1)


def gate_norm(y, zgate, norm_gain, groups):
    rows = y.shape[0]
    gated = y * jax.nn.silu(zgate.astype(jnp.float32))
    blocks = gated.reshape(rows, groups, -1)
    meansq = jnp.mean(blocks * blocks, axis=-1, keepdims=True)
    normed = (blocks * lax.rsqrt(meansq + 1e-05)).reshape(rows, -1) * norm_gain[None, :]
    return normed.astype(jnp.bfloat16)


def mixer_layer(
    xs,
    bc,
    zgate,
    dt_raw,
    dt_bias,
    a_log,
    d_skip,
    norm_gain,
    resid,
    w_out,
    final_gain,
    head_weight,
    lengths,
):
    rows = xs.shape[0]
    inner = xs.shape[1]
    seq_count = lax.axis_size("seq")
    place = lax.axis_index("seq")
    heads_all = a_log.shape[0]
    heads = heads_all // seq_count
    groups = NGROUPS // seq_count
    group_rows = rows * seq_count

    lens = lengths[0]
    slots = lens.shape[0]
    ends = jnp.cumsum(lens)
    positions = jnp.arange(group_rows, dtype=jnp.int32)
    segment = jnp.sum((positions[:, None] >= ends[None, :]).astype(jnp.int32), axis=1)
    live = segment < slots
    group_pos = jnp.arange(group_rows, dtype=jnp.int32)
    picker = (group_pos[None, :] == (ends - 1)[:, None]).astype(jnp.bfloat16)

    width = resid.shape[1]
    w_cols = lax.dynamic_slice_in_dim(w_out, place * width, width, axis=1)
    w_full = lax.all_gather(w_cols, "req", axis=0, tiled=True)
    w_blocks = w_full.reshape(seq_count, groups, inner // NGROUPS, width)

    block_cols = inner // NGROUPS
    block_heads = heads // groups

    def by_dest(part, width_of, half):
        piece = part.reshape(rows, seq_count, groups, width_of)[:, :, half, :]
        return piece.transpose(1, 0, 2)

    moves = []
    for half in range(groups):
        packed = jnp.concatenate(
            [
                by_dest(xs, block_cols, half),
                by_dest(zgate, block_cols, half),
                by_dest(bc[:, : NGROUPS * STATE], STATE, half),
                by_dest(bc[:, NGROUPS * STATE :], STATE, half),
                by_dest(dt_raw, block_heads, half),
            ],
            axis=2,
        )
        moves.append(lax.all_to_all(packed, "seq", split_axis=0, concat_axis=0, tiled=True))

    gated_parts = []
    picked_parts = []
    for half in range(groups):
        moved = moves[half]
        if half > 0:
            moved = lax.optimization_barrier((moved, gated, picked_parts[-1]))[0]
        moved = moved.reshape(group_rows, -1)
        xg = moved[:, :block_cols]
        zg = moved[:, block_cols : 2 * block_cols]
        bg = moved[:, 2 * block_cols : 2 * block_cols + STATE]
        cg = moved[:, 2 * block_cols + STATE : 2 * block_cols + 2 * STATE]
        dg = moved[:, 2 * block_cols + 2 * STATE :]

        first_head = (place * groups + half) * block_heads
        my_heads = lambda v: lax.dynamic_slice_in_dim(v, first_head, block_heads)
        rate = jnp.exp(my_heads(a_log))
        skipw = my_heads(d_skip)
        steps_dt = jax.nn.softplus(dg.astype(jnp.float32) + my_heads(dt_bias)[None, :])

        state_in = jnp.zeros((block_heads, HEAD_DIM, STATE), jnp.float32)
        prev_seg = jnp.array(-1, jnp.int32)
        ys = []
        for chunk in range(seq_count):
            lo, hi = chunk * rows, (chunk + 1) * rows
            local, keep, state, carry_w, cmat = block_terms(
                xg[lo:hi], bg[lo:hi], cg[lo:hi], steps_dt[lo:hi], segment[lo:hi], live[lo:hi],
                prev_seg, rate, skipw, 1,
            )
            y4 = (local + carry_term(state_in, cmat, carry_w, 1)) * live[lo:hi].astype(
                jnp.float32
            )[:, None, None, None]
            ys.append(y4.reshape(rows, block_cols))
            state_in = keep[:, None, None] * state_in + state
            prev_seg = segment[hi - 1]
        y = jnp.concatenate(ys, axis=0)
        gain = lax.dynamic_slice_in_dim(norm_gain, (place * groups + half) * block_cols, block_cols)
        gated = gate_norm(y, zg, gain, 1)
        gated_parts.append(lax.all_gather(gated, "seq", axis=1, tiled=True))
        picked = jnp.dot(picker, gated, preferred_element_type=jnp.float32).astype(jnp.bfloat16)
        picked = lax.all_gather(picked, "seq", axis=1, tiled=True)
        picked_parts.append(
            jnp.dot(picked, w_blocks[:, half].reshape(-1, width), preferred_element_type=jnp.float32)
        )

    picked_resid = jnp.dot(picker, resid, preferred_element_type=jnp.float32)
    picked_mixer = sum(picked_parts)
    picked_rows = (
        picked_resid + picked_mixer.astype(jnp.bfloat16).astype(jnp.float32)
    ).astype(jnp.bfloat16)
    row_pair = lax.all_gather(picked_rows, "seq", axis=1, tiled=True)
    collected = lax.all_gather(row_pair, "req", axis=0, tiled=True)
    last_rows = collected.astype(jnp.float32)
    meansq = jnp.mean(last_rows * last_rows, axis=-1, keepdims=True)
    normed = (last_rows * lax.rsqrt(meansq + 1e-05) * final_gain[None, :]).astype(jnp.bfloat16)
    logits = jnp.dot(normed, head_weight, preferred_element_type=jnp.float32)

    mixer_f32 = None
    for half in range(groups):
        part = jnp.dot(gated_parts[half], w_blocks[:, half].reshape(-1, width),
                       preferred_element_type=jnp.float32)
        mixer_f32 = part if mixer_f32 is None else mixer_f32 + part
    mixer = mixer_f32.astype(jnp.bfloat16)
    layer_out = (resid.astype(jnp.float32) + mixer.astype(jnp.float32)).astype(jnp.bfloat16)
    return (layer_out, logits)


def solution(mesh):
    placed = (
        P(("req", "seq"), None),
        P(("req", "seq"), None),
        P(("req", "seq"), None),
        P(("req", "seq"), None),
        P(),
        P(),
        P(),
        P(),
        P("req", "seq"),
        P("req", None),
        P(),
        P(None, ("req", "seq")),
        P("req", None),
    )
    return jax.shard_map(
        mixer_layer,
        mesh=mesh,
        in_specs=placed,
        out_specs=(P("req", "seq"), P(None, ("req", "seq"))),
        check_vma=False,
    )
```

```python
import jax
import jax.numpy as jnp
from jax import lax
from jax.sharding import PartitionSpec as P

HEAD_DIM = 64
NGROUPS = 8
STATE = 128


def split_halves(value):
    upper = value.astype(jnp.bfloat16)
    lower = (value - upper.astype(jnp.float32)).astype(jnp.bfloat16)
    return (upper, lower)


def group_inner(operands):
    cum_g, scores_g, inflow_g, x_g, allowed_mask = operands
    diff = cum_g[:, None, :] - cum_g[None, :, :]
    decay = jnp.where(allowed_mask[:, :, None], jnp.exp(jnp.minimum(diff, 0.0)), 0.0)
    weights = decay * scores_g[:, :, None] * inflow_g[None, :, :]
    upper, lower = split_halves(weights)
    first_part = jnp.einsum("tsk,skp->tkp", upper, x_g, preferred_element_type=jnp.float32)
    second_part = jnp.einsum("tsk,skp->tkp", lower, x_g, preferred_element_type=jnp.float32)
    return first_part + second_part


def block_terms(xb, bb, cb, dtb, segment, live, prev_seg, rate, d_skip, groups):
    rows = xb.shape[0]
    heads = rate.shape[0]
    per_group = heads // groups
    x4 = xb.reshape(rows, groups, per_group, HEAD_DIM)
    bmat = bb.reshape(rows, groups, STATE)
    cmat = cb.reshape(rows, groups, STATE)
    livef = live.astype(jnp.float32)
    cum = jnp.cumsum(-rate[None, :] * dtb, axis=0)
    inflow = dtb * livef[:, None]
    index = jnp.arange(rows, dtype=jnp.int32)
    allowed_mask = (segment[:, None] == segment[None, :]) & (index[:, None] >= index[None, :])
    scores = jnp.einsum("tgn,sgn->gts", cmat, bmat, preferred_element_type=jnp.float32)
    cum_g = cum.reshape(rows, groups, per_group).transpose(1, 0, 2)
    inflow_g = inflow.reshape(rows, groups, per_group).transpose(1, 0, 2)
    x_g = x4.transpose(1, 0, 2, 3)
    allowed_all = jnp.broadcast_to(allowed_mask[None], (groups, rows, rows))
    y_groups = lax.map(group_inner, (cum_g, scores, inflow_g, x_g, allowed_all))
    y_inner = y_groups.transpose(1, 0, 2, 3)
    skip = d_skip.reshape(1, groups, per_group, 1) * x4.astype(jnp.float32)
    last_seg = segment[rows - 1]
    tail = (
        jnp.exp(cum[rows - 1][None, :] - cum)
        * (segment == last_seg).astype(jnp.float32)[:, None]
        * inflow
    )
    scaled = tail.reshape(rows, groups, per_group, 1) * x4.astype(jnp.float32)
    upper, lower = split_halves(scaled)
    state = jnp.einsum("sgkp,sgn->gkpn", upper, bmat, preferred_element_type=jnp.float32)
    state = state + jnp.einsum("sgkp,sgn->gkpn", lower, bmat, preferred_element_type=jnp.float32)
    keep = jnp.exp(cum[rows - 1]) * (last_seg == prev_seg).astype(jnp.float32)
    carry_w = jnp.exp(cum) * (segment == prev_seg).astype(jnp.float32)[:, None]
    return (y_inner + skip, keep, state.reshape(heads, HEAD_DIM, STATE), carry_w, cmat)


def carry_term(arriving_vector, cmat, carry_w, groups):
    rows = cmat.shape[0]
    heads = arriving_vector.shape[0]
    per_group = heads // groups
    state4 = arriving_vector.reshape(groups, per_group, HEAD_DIM, STATE)
    upper, lower = split_halves(state4)
    y_carry = jnp.einsum("tgn,gkpn->tgkp", cmat, upper, preferred_element_type=jnp.float32)
    y_carry = y_carry + jnp.einsum(
        "tgn,gkpn->tgkp", cmat, lower, preferred_element_type=jnp.float32
    )
    return y_carry * carry_w.reshape(rows, groups, per_group, 1)


def gate_norm(y, zgate, norm_gain, groups):
    rows = y.shape[0]
    gated = y * jax.nn.silu(zgate.astype(jnp.float32))
    blocks = gated.reshape(rows, groups, -1)
    meansq = jnp.mean(blocks * blocks, axis=-1, keepdims=True)
    normed = (blocks * lax.rsqrt(meansq + 1e-05)).reshape(rows, -1) * norm_gain[None, :]
    return normed.astype(jnp.bfloat16)


def mixer_layer(
    xs,
    bc,
    zgate,
    dt_raw,
    dt_bias,
    a_log,
    d_skip,
    norm_gain,
    resid,
    w_out,
    final_gain,
    head_weight,
    lengths,
):
    rows = xs.shape[0]
    inner = xs.shape[1]
    seq_count = lax.axis_size("seq")
    place = lax.axis_index("seq")
    heads_all = a_log.shape[0]
    heads = heads_all // seq_count
    groups = NGROUPS // seq_count
    group_rows = rows * seq_count

    lens = lengths[0]
    slots = lens.shape[0]
    ends = jnp.cumsum(lens)
    positions = jnp.arange(group_rows, dtype=jnp.int32)
    segment = jnp.sum((positions[:, None] >= ends[None, :]).astype(jnp.int32), axis=1)
    live = segment < slots
    group_pos = jnp.arange(group_rows, dtype=jnp.int32)
    picker = (group_pos[None, :] == (ends - 1)[:, None]).astype(jnp.bfloat16)

    width = resid.shape[1]
    w_cols = lax.dynamic_slice_in_dim(w_out, place * width, width, axis=1)
    w_full = lax.all_gather(w_cols, "req", axis=0, tiled=True)
    w_blocks = w_full.reshape(seq_count, groups, inner // NGROUPS, width)

    block_cols = inner // NGROUPS
    block_heads = heads // groups

    def by_dest(part, width_of, half):
        piece = part.reshape(rows, seq_count, groups, width_of)[:, :, half, :]
        return piece.transpose(1, 0, 2)

    moves = []
    for half in range(groups):
        packed = jnp.concatenate(
            [
                by_dest(xs, block_cols, half),
                by_dest(zgate, block_cols, half),
                by_dest(bc[:, : NGROUPS * STATE], STATE, half),
                by_dest(bc[:, NGROUPS * STATE :], STATE, half),
                by_dest(dt_raw, block_heads, half),
            ],
            axis=2,
        )
        moves.append(lax.all_to_all(packed, "seq", split_axis=0, concat_axis=0, tiled=True))

    gated_parts = []
    picked_parts = []
    for half in range(groups):
        moved = moves[half]
        if half > 0:
            moved = lax.optimization_barrier((moved, gated))[0]
        moved = moved.reshape(group_rows, -1)
        xg = moved[:, :block_cols]
        zg = moved[:, block_cols : 2 * block_cols]
        bg = moved[:, 2 * block_cols : 2 * block_cols + STATE]
        cg = moved[:, 2 * block_cols + STATE : 2 * block_cols + 2 * STATE]
        dg = moved[:, 2 * block_cols + 2 * STATE :]

        first_head = (place * groups + half) * block_heads
        my_heads = lambda v: lax.dynamic_slice_in_dim(v, first_head, block_heads)
        rate = jnp.exp(my_heads(a_log))
        skipw = my_heads(d_skip)
        steps_dt = jax.nn.softplus(dg.astype(jnp.float32) + my_heads(dt_bias)[None, :])

        state_in = jnp.zeros((block_heads, HEAD_DIM, STATE), jnp.float32)
        prev_seg = jnp.array(-1, jnp.int32)
        ys = []
        for chunk in range(seq_count):
            lo, hi = chunk * rows, (chunk + 1) * rows
            local, keep, state, carry_w, cmat = block_terms(
                xg[lo:hi], bg[lo:hi], cg[lo:hi], steps_dt[lo:hi], segment[lo:hi], live[lo:hi],
                prev_seg, rate, skipw, 1,
            )
            y4 = (local + carry_term(state_in, cmat, carry_w, 1)) * live[lo:hi].astype(
                jnp.float32
            )[:, None, None, None]
            ys.append(y4.reshape(rows, block_cols))
            state_in = keep[:, None, None] * state_in + state
            prev_seg = segment[hi - 1]
        y = jnp.concatenate(ys, axis=0)
        gain = lax.dynamic_slice_in_dim(norm_gain, (place * groups + half) * block_cols, block_cols)
        gated = gate_norm(y, zg, gain, 1)
        gated_parts.append(lax.all_gather(gated, "seq", axis=1, tiled=True))
        picked_parts.append(
            jnp.dot(picker, gated, preferred_element_type=jnp.float32).astype(jnp.bfloat16)
        )

    picked_resid = jnp.dot(picker, resid, preferred_element_type=jnp.float32)
    picked = lax.all_gather(jnp.stack(picked_parts, axis=1), "seq", axis=0)
    picked_mixer = jnp.einsum("sthj,shjo->to", picked, w_blocks, preferred_element_type=jnp.float32)
    picked_rows = (
        picked_resid + picked_mixer.astype(jnp.bfloat16).astype(jnp.float32)
    ).astype(jnp.bfloat16)
    row_pair = lax.all_gather(picked_rows, "seq", axis=1, tiled=True)
    collected = lax.all_gather(row_pair, "req", axis=0, tiled=True)
    last_rows = collected.astype(jnp.float32)
    meansq = jnp.mean(last_rows * last_rows, axis=-1, keepdims=True)
    normed = (last_rows * lax.rsqrt(meansq + 1e-05) * final_gain[None, :]).astype(jnp.bfloat16)
    logits = jnp.dot(normed, head_weight, preferred_element_type=jnp.float32)

    mixer_f32 = None
    for half in range(groups):
        part = jnp.dot(gated_parts[half], w_blocks[:, half].reshape(-1, width),
                       preferred_element_type=jnp.float32)
        mixer_f32 = part if mixer_f32 is None else mixer_f32 + part
    mixer = mixer_f32.astype(jnp.bfloat16)
    layer_out = (resid.astype(jnp.float32) + mixer.astype(jnp.float32)).astype(jnp.bfloat16)
    return (layer_out, logits)


def solution(mesh):
    placed = (
        P(("req", "seq"), None),
        P(("req", "seq"), None),
        P(("req", "seq"), None),
        P(("req", "seq"), None),
        P(),
        P(),
        P(),
        P(),
        P("req", "seq"),
        P("req", None),
        P(),
        P(None, ("req", "seq")),
        P("req", None),
    )
    return jax.shard_map(
        mixer_layer,
        mesh=mesh,
        in_specs=placed,
        out_specs=(P("req", "seq"), P(None, ("req", "seq"))),
        check_vma=False,
    )
```

```python
import jax
import jax.numpy as jnp
from jax import lax
from jax.sharding import PartitionSpec as P

HEAD_DIM = 64
NGROUPS = 8
STATE = 128


def split_halves(value):
    upper = value.astype(jnp.bfloat16)
    lower = (value - upper.astype(jnp.float32)).astype(jnp.bfloat16)
    return (upper, lower)


def group_inner(operands):
    cum_g, scores_g, inflow_g, x_g, allowed_mask = operands
    diff = cum_g[:, None, :] - cum_g[None, :, :]
    decay = jnp.where(allowed_mask[:, :, None], jnp.exp(jnp.minimum(diff, 0.0)), 0.0)
    weights = decay * scores_g[:, :, None] * inflow_g[None, :, :]
    upper, lower = split_halves(weights)
    first_part = jnp.einsum("tsk,skp->tkp", upper, x_g, preferred_element_type=jnp.float32)
    second_part = jnp.einsum("tsk,skp->tkp", lower, x_g, preferred_element_type=jnp.float32)
    return first_part + second_part


def block_terms(xb, bb, cb, dtb, segment, live, prev_seg, rate, d_skip, groups):
    rows = xb.shape[0]
    heads = rate.shape[0]
    per_group = heads // groups
    x4 = xb.reshape(rows, groups, per_group, HEAD_DIM)
    bmat = bb.reshape(rows, groups, STATE)
    cmat = cb.reshape(rows, groups, STATE)
    livef = live.astype(jnp.float32)
    cum = jnp.cumsum(-rate[None, :] * dtb, axis=0)
    inflow = dtb * livef[:, None]
    index = jnp.arange(rows, dtype=jnp.int32)
    allowed_mask = (segment[:, None] == segment[None, :]) & (index[:, None] >= index[None, :])
    scores = jnp.einsum("tgn,sgn->gts", cmat, bmat, preferred_element_type=jnp.float32)
    cum_g = cum.reshape(rows, groups, per_group).transpose(1, 0, 2)
    inflow_g = inflow.reshape(rows, groups, per_group).transpose(1, 0, 2)
    x_g = x4.transpose(1, 0, 2, 3)
    allowed_all = jnp.broadcast_to(allowed_mask[None], (groups, rows, rows))
    y_groups = lax.map(group_inner, (cum_g, scores, inflow_g, x_g, allowed_all))
    y_inner = y_groups.transpose(1, 0, 2, 3)
    skip = d_skip.reshape(1, groups, per_group, 1) * x4.astype(jnp.float32)
    last_seg = segment[rows - 1]
    tail = (
        jnp.exp(cum[rows - 1][None, :] - cum)
        * (segment == last_seg).astype(jnp.float32)[:, None]
        * inflow
    )
    scaled = tail.reshape(rows, groups, per_group, 1) * x4.astype(jnp.float32)
    upper, lower = split_halves(scaled)
    state = jnp.einsum("sgkp,sgn->gkpn", upper, bmat, preferred_element_type=jnp.float32)
    state = state + jnp.einsum("sgkp,sgn->gkpn", lower, bmat, preferred_element_type=jnp.float32)
    keep = jnp.exp(cum[rows - 1]) * (last_seg == prev_seg).astype(jnp.float32)
    carry_w = jnp.exp(cum) * (segment == prev_seg).astype(jnp.float32)[:, None]
    return (y_inner + skip, keep, state.reshape(heads, HEAD_DIM, STATE), carry_w, cmat)


def carry_term(arriving_vector, cmat, carry_w, groups):
    rows = cmat.shape[0]
    heads = arriving_vector.shape[0]
    per_group = heads // groups
    state4 = arriving_vector.reshape(groups, per_group, HEAD_DIM, STATE)
    upper, lower = split_halves(state4)
    y_carry = jnp.einsum("tgn,gkpn->tgkp", cmat, upper, preferred_element_type=jnp.float32)
    y_carry = y_carry + jnp.einsum(
        "tgn,gkpn->tgkp", cmat, lower, preferred_element_type=jnp.float32
    )
    return y_carry * carry_w.reshape(rows, groups, per_group, 1)


def gate_norm(y, zgate, norm_gain, groups):
    rows = y.shape[0]
    gated = y * jax.nn.silu(zgate.astype(jnp.float32))
    blocks = gated.reshape(rows, groups, -1)
    meansq = jnp.mean(blocks * blocks, axis=-1, keepdims=True)
    normed = (blocks * lax.rsqrt(meansq + 1e-05)).reshape(rows, -1) * norm_gain[None, :]
    return normed.astype(jnp.bfloat16)


def gather_by_shifts(value, axis):
    count, mine = lax.axis_size(axis), lax.axis_index(axis)
    parts = [value]
    for shift in range(1, count):
        pairs = [(i, (i + shift) % count) for i in range(count)]
        parts.append(lax.ppermute(value, axis, perm=pairs))
    order = (mine - jnp.arange(count, dtype=jnp.int32)) % count
    return jnp.take(jnp.stack(parts), order, axis=0)


def gather_by_doubling(value, axis):
    count, mine = lax.axis_size(axis), lax.axis_index(axis)
    acc = value[None]
    step = 1
    while step < count:
        pairs = [(i, i ^ step) for i in range(count)]
        other = lax.ppermute(acc, axis, perm=pairs)
        low = (mine // step) % 2 == 0
        acc = jnp.where(low, jnp.concatenate([acc, other]), jnp.concatenate([other, acc]))
        step *= 2
    return acc


def mixer_layer(
    xs,
    bc,
    zgate,
    dt_raw,
    dt_bias,
    a_log,
    d_skip,
    norm_gain,
    resid,
    w_out,
    final_gain,
    head_weight,
    lengths,
):
    rows = xs.shape[0]
    inner = xs.shape[1]
    seq_count = lax.axis_size("seq")
    place = lax.axis_index("seq")
    heads_all = a_log.shape[0]
    heads = heads_all // seq_count
    groups = NGROUPS // seq_count
    group_rows = rows * seq_count

    lens = lengths[0]
    slots = lens.shape[0]
    ends = jnp.cumsum(lens)
    positions = jnp.arange(group_rows, dtype=jnp.int32)
    segment = jnp.sum((positions[:, None] >= ends[None, :]).astype(jnp.int32), axis=1)
    live = segment < slots
    group_pos = jnp.arange(group_rows, dtype=jnp.int32)
    picker = (group_pos[None, :] == (ends - 1)[:, None]).astype(jnp.bfloat16)

    width = resid.shape[1]
    w_cols = lax.dynamic_slice_in_dim(w_out, place * width, width, axis=1)
    w_full = lax.all_gather(w_cols, "req", axis=0, tiled=True)
    w_blocks = w_full.reshape(seq_count, groups, inner // NGROUPS, width)

    block_cols = inner // NGROUPS
    block_heads = heads // groups

    def by_dest(part, width_of, half):
        piece = part.reshape(rows, seq_count, groups, width_of)[:, :, half, :]
        return piece.transpose(1, 0, 2)

    moves = []
    for half in range(groups):
        packed = jnp.concatenate(
            [
                by_dest(xs, block_cols, half),
                by_dest(zgate, block_cols, half),
                by_dest(bc[:, : NGROUPS * STATE], STATE, half),
                by_dest(bc[:, NGROUPS * STATE :], STATE, half),
                by_dest(dt_raw, block_heads, half),
            ],
            axis=2,
        )
        moves.append(lax.all_to_all(packed, "seq", split_axis=0, concat_axis=0, tiled=True))

    gated_parts = []
    picked_parts = []
    for half in range(groups):
        moved = moves[half]
        if half > 0:
            moved = lax.optimization_barrier((moved, gated))[0]
        moved = moved.reshape(group_rows, -1)
        xg = moved[:, :block_cols]
        zg = moved[:, block_cols : 2 * block_cols]
        bg = moved[:, 2 * block_cols : 2 * block_cols + STATE]
        cg = moved[:, 2 * block_cols + STATE : 2 * block_cols + 2 * STATE]
        dg = moved[:, 2 * block_cols + 2 * STATE :]

        first_head = (place * groups + half) * block_heads
        my_heads = lambda v: lax.dynamic_slice_in_dim(v, first_head, block_heads)
        rate = jnp.exp(my_heads(a_log))
        skipw = my_heads(d_skip)
        steps_dt = jax.nn.softplus(dg.astype(jnp.float32) + my_heads(dt_bias)[None, :])

        state_in = jnp.zeros((block_heads, HEAD_DIM, STATE), jnp.float32)
        prev_seg = jnp.array(-1, jnp.int32)
        ys = []
        for chunk in range(seq_count):
            lo, hi = chunk * rows, (chunk + 1) * rows
            local, keep, state, carry_w, cmat = block_terms(
                xg[lo:hi], bg[lo:hi], cg[lo:hi], steps_dt[lo:hi], segment[lo:hi], live[lo:hi],
                prev_seg, rate, skipw, 1,
            )
            y4 = (local + carry_term(state_in, cmat, carry_w, 1)) * live[lo:hi].astype(
                jnp.float32
            )[:, None, None, None]
            ys.append(y4.reshape(rows, block_cols))
            state_in = keep[:, None, None] * state_in + state
            prev_seg = segment[hi - 1]
        y = jnp.concatenate(ys, axis=0)
        gain = lax.dynamic_slice_in_dim(norm_gain, (place * groups + half) * block_cols, block_cols)
        gated = gate_norm(y, zg, gain, 1)
        gated_parts.append(lax.all_gather(gated, "seq", axis=1, tiled=True))
        picked_parts.append(
            jnp.dot(picker, gated, preferred_element_type=jnp.float32).astype(jnp.bfloat16)
        )

    picked_resid = jnp.dot(picker, resid, preferred_element_type=jnp.float32)
    picked = gather_by_shifts(jnp.stack(picked_parts, axis=1), "seq")
    picked_mixer = jnp.einsum("sthj,shjo->to", picked, w_blocks, preferred_element_type=jnp.float32)
    picked_rows = (
        picked_resid + picked_mixer.astype(jnp.bfloat16).astype(jnp.float32)
    ).astype(jnp.bfloat16)
    row_pair = gather_by_shifts(picked_rows, "seq").transpose(1, 0, 2).reshape(slots, -1)
    collected = gather_by_doubling(row_pair, "req")
    last_rows = collected.reshape(-1, seq_count * width).astype(jnp.float32)
    meansq = jnp.mean(last_rows * last_rows, axis=-1, keepdims=True)
    normed = (last_rows * lax.rsqrt(meansq + 1e-05) * final_gain[None, :]).astype(jnp.bfloat16)
    logits = jnp.dot(normed, head_weight, preferred_element_type=jnp.float32)

    mixer_f32 = None
    for half in range(groups):
        part = jnp.dot(gated_parts[half], w_blocks[:, half].reshape(-1, width),
                       preferred_element_type=jnp.float32)
        mixer_f32 = part if mixer_f32 is None else mixer_f32 + part
    mixer = mixer_f32.astype(jnp.bfloat16)
    layer_out = (resid.astype(jnp.float32) + mixer.astype(jnp.float32)).astype(jnp.bfloat16)
    return (layer_out, logits)


def solution(mesh):
    placed = (
        P(("req", "seq"), None),
        P(("req", "seq"), None),
        P(("req", "seq"), None),
        P(("req", "seq"), None),
        P(),
        P(),
        P(),
        P(),
        P("req", "seq"),
        P("req", None),
        P(),
        P(None, ("req", "seq")),
        P("req", None),
    )
    return jax.shard_map(
        mixer_layer,
        mesh=mesh,
        in_specs=placed,
        out_specs=(P("req", "seq"), P(None, ("req", "seq"))),
        check_vma=False,
    )
```

```python
import jax
import jax.numpy as jnp
from jax import lax
from jax.sharding import PartitionSpec as P

HEAD_DIM = 64
NGROUPS = 8
STATE = 128


def split_halves(value):
    upper = value.astype(jnp.bfloat16)
    lower = (value - upper.astype(jnp.float32)).astype(jnp.bfloat16)
    return (upper, lower)


def group_inner(operands):
    cum_g, scores_g, inflow_g, x_g, allowed_mask = operands
    diff = cum_g[:, None, :] - cum_g[None, :, :]
    decay = jnp.where(allowed_mask[:, :, None], jnp.exp(jnp.minimum(diff, 0.0)), 0.0)
    weights = decay * scores_g[:, :, None] * inflow_g[None, :, :]
    upper, lower = split_halves(weights)
    first_part = jnp.einsum("tsk,skp->tkp", upper, x_g, preferred_element_type=jnp.float32)
    second_part = jnp.einsum("tsk,skp->tkp", lower, x_g, preferred_element_type=jnp.float32)
    return first_part + second_part


def block_terms(xb, bb, cb, dtb, segment, live, prev_seg, rate, d_skip, groups):
    rows = xb.shape[0]
    heads = rate.shape[0]
    per_group = heads // groups
    x4 = xb.reshape(rows, groups, per_group, HEAD_DIM)
    bmat = bb.reshape(rows, groups, STATE)
    cmat = cb.reshape(rows, groups, STATE)
    livef = live.astype(jnp.float32)
    cum = jnp.cumsum(-rate[None, :] * dtb, axis=0)
    inflow = dtb * livef[:, None]
    index = jnp.arange(rows, dtype=jnp.int32)
    allowed_mask = (segment[:, None] == segment[None, :]) & (index[:, None] >= index[None, :])
    scores = jnp.einsum("tgn,sgn->gts", cmat, bmat, preferred_element_type=jnp.float32)
    cum_g = cum.reshape(rows, groups, per_group).transpose(1, 0, 2)
    inflow_g = inflow.reshape(rows, groups, per_group).transpose(1, 0, 2)
    x_g = x4.transpose(1, 0, 2, 3)
    allowed_all = jnp.broadcast_to(allowed_mask[None], (groups, rows, rows))
    y_groups = lax.map(group_inner, (cum_g, scores, inflow_g, x_g, allowed_all))
    y_inner = y_groups.transpose(1, 0, 2, 3)
    skip = d_skip.reshape(1, groups, per_group, 1) * x4.astype(jnp.float32)
    last_seg = segment[rows - 1]
    tail = (
        jnp.exp(cum[rows - 1][None, :] - cum)
        * (segment == last_seg).astype(jnp.float32)[:, None]
        * inflow
    )
    scaled = tail.reshape(rows, groups, per_group, 1) * x4.astype(jnp.float32)
    upper, lower = split_halves(scaled)
    state = jnp.einsum("sgkp,sgn->gkpn", upper, bmat, preferred_element_type=jnp.float32)
    state = state + jnp.einsum("sgkp,sgn->gkpn", lower, bmat, preferred_element_type=jnp.float32)
    keep = jnp.exp(cum[rows - 1]) * (last_seg == prev_seg).astype(jnp.float32)
    carry_w = jnp.exp(cum) * (segment == prev_seg).astype(jnp.float32)[:, None]
    return (y_inner + skip, keep, state.reshape(heads, HEAD_DIM, STATE), carry_w, cmat)


def carry_term(arriving_vector, cmat, carry_w, groups):
    rows = cmat.shape[0]
    heads = arriving_vector.shape[0]
    per_group = heads // groups
    state4 = arriving_vector.reshape(groups, per_group, HEAD_DIM, STATE)
    upper, lower = split_halves(state4)
    y_carry = jnp.einsum("tgn,gkpn->tgkp", cmat, upper, preferred_element_type=jnp.float32)
    y_carry = y_carry + jnp.einsum(
        "tgn,gkpn->tgkp", cmat, lower, preferred_element_type=jnp.float32
    )
    return y_carry * carry_w.reshape(rows, groups, per_group, 1)


def gate_norm(y, zgate, norm_gain, groups):
    rows = y.shape[0]
    gated = y * jax.nn.silu(zgate.astype(jnp.float32))
    blocks = gated.reshape(rows, groups, -1)
    meansq = jnp.mean(blocks * blocks, axis=-1, keepdims=True)
    normed = (blocks * lax.rsqrt(meansq + 1e-05)).reshape(rows, -1) * norm_gain[None, :]
    return normed.astype(jnp.bfloat16)


def gather_by_shifts(value, axis):
    count, mine = lax.axis_size(axis), lax.axis_index(axis)
    parts = [value]
    for shift in range(1, count):
        pairs = [(i, (i + shift) % count) for i in range(count)]
        parts.append(lax.ppermute(value, axis, perm=pairs))
    order = (mine - jnp.arange(count, dtype=jnp.int32)) % count
    return jnp.take(jnp.stack(parts), order, axis=0)


def all_to_all_by_shifts(value, axis):
    count, mine = lax.axis_size(axis), lax.axis_index(axis)
    parts = [lax.dynamic_index_in_dim(value, mine, 0, keepdims=False)]
    for shift in range(1, count):
        pairs = [(i, (i + shift) % count) for i in range(count)]
        piece = lax.dynamic_index_in_dim(value, (mine + shift) % count, 0, keepdims=False)
        parts.append(lax.ppermute(piece, axis, perm=pairs))
    order = (mine - jnp.arange(count, dtype=jnp.int32)) % count
    return jnp.take(jnp.stack(parts), order, axis=0)


def gather_by_doubling(value, axis):
    count, mine = lax.axis_size(axis), lax.axis_index(axis)
    acc = value[None]
    step = 1
    while step < count:
        pairs = [(i, i ^ step) for i in range(count)]
        other = lax.ppermute(acc, axis, perm=pairs)
        low = (mine // step) % 2 == 0
        acc = jnp.where(low, jnp.concatenate([acc, other]), jnp.concatenate([other, acc]))
        step *= 2
    return acc


def mixer_layer(
    xs,
    bc,
    zgate,
    dt_raw,
    dt_bias,
    a_log,
    d_skip,
    norm_gain,
    resid,
    w_out,
    final_gain,
    head_weight,
    lengths,
):
    rows = xs.shape[0]
    inner = xs.shape[1]
    seq_count = lax.axis_size("seq")
    place = lax.axis_index("seq")
    heads_all = a_log.shape[0]
    heads = heads_all // seq_count
    groups = NGROUPS // seq_count
    group_rows = rows * seq_count

    lens = lengths[0]
    slots = lens.shape[0]
    ends = jnp.cumsum(lens)
    positions = jnp.arange(group_rows, dtype=jnp.int32)
    segment = jnp.sum((positions[:, None] >= ends[None, :]).astype(jnp.int32), axis=1)
    live = segment < slots
    group_pos = jnp.arange(group_rows, dtype=jnp.int32)
    picker = (group_pos[None, :] == (ends - 1)[:, None]).astype(jnp.bfloat16)

    width = resid.shape[1]
    w_cols = lax.dynamic_slice_in_dim(w_out, place * width, width, axis=1)
    w_full = lax.all_gather(w_cols, "req", axis=0, tiled=True)
    w_blocks = w_full.reshape(seq_count, groups, inner // NGROUPS, width)

    block_cols = inner // NGROUPS
    block_heads = heads // groups

    def by_dest(part, width_of, half):
        piece = part.reshape(rows, seq_count, groups, width_of)[:, :, half, :]
        return piece.transpose(1, 0, 2)

    moves = []
    for half in range(groups):
        packed = jnp.concatenate(
            [
                by_dest(xs, block_cols, half),
                by_dest(zgate, block_cols, half),
                by_dest(bc[:, : NGROUPS * STATE], STATE, half),
                by_dest(bc[:, NGROUPS * STATE :], STATE, half),
                by_dest(dt_raw, block_heads, half),
            ],
            axis=2,
        )
        if moves:
            packed = lax.optimization_barrier((packed, moves[-1]))[0]
        moves.append(all_to_all_by_shifts(packed, "seq"))

    gated_parts = []
    picked_parts = []
    for half in range(groups):
        moved = moves[half]
        if half > 0:
            moved = lax.optimization_barrier((moved, gated))[0]
        moved = moved.reshape(group_rows, -1)
        xg = moved[:, :block_cols]
        zg = moved[:, block_cols : 2 * block_cols]
        bg = moved[:, 2 * block_cols : 2 * block_cols + STATE]
        cg = moved[:, 2 * block_cols + STATE : 2 * block_cols + 2 * STATE]
        dg = moved[:, 2 * block_cols + 2 * STATE :]

        first_head = (place * groups + half) * block_heads
        my_heads = lambda v: lax.dynamic_slice_in_dim(v, first_head, block_heads)
        rate = jnp.exp(my_heads(a_log))
        skipw = my_heads(d_skip)
        steps_dt = jax.nn.softplus(dg.astype(jnp.float32) + my_heads(dt_bias)[None, :])

        state_in = jnp.zeros((block_heads, HEAD_DIM, STATE), jnp.float32)
        prev_seg = jnp.array(-1, jnp.int32)
        ys = []
        for chunk in range(seq_count):
            lo, hi = chunk * rows, (chunk + 1) * rows
            local, keep, state, carry_w, cmat = block_terms(
                xg[lo:hi], bg[lo:hi], cg[lo:hi], steps_dt[lo:hi], segment[lo:hi], live[lo:hi],
                prev_seg, rate, skipw, 1,
            )
            y4 = (local + carry_term(state_in, cmat, carry_w, 1)) * live[lo:hi].astype(
                jnp.float32
            )[:, None, None, None]
            ys.append(y4.reshape(rows, block_cols))
            state_in = keep[:, None, None] * state_in + state
            prev_seg = segment[hi - 1]
        y = jnp.concatenate(ys, axis=0)
        gain = lax.dynamic_slice_in_dim(norm_gain, (place * groups + half) * block_cols, block_cols)
        gated = gate_norm(y, zg, gain, 1)
        gated_parts.append(lax.all_gather(gated, "seq", axis=1, tiled=True))
        picked_parts.append(
            jnp.dot(picker, gated, preferred_element_type=jnp.float32).astype(jnp.bfloat16)
        )

    picked_resid = jnp.dot(picker, resid, preferred_element_type=jnp.float32)
    picked = gather_by_shifts(jnp.stack(picked_parts, axis=1), "seq")
    picked_mixer = jnp.einsum("sthj,shjo->to", picked, w_blocks, preferred_element_type=jnp.float32)
    picked_rows = (
        picked_resid + picked_mixer.astype(jnp.bfloat16).astype(jnp.float32)
    ).astype(jnp.bfloat16)
    row_pair = gather_by_shifts(picked_rows, "seq").transpose(1, 0, 2).reshape(slots, -1)
    collected = gather_by_doubling(row_pair, "req")
    last_rows = collected.reshape(-1, seq_count * width).astype(jnp.float32)
    meansq = jnp.mean(last_rows * last_rows, axis=-1, keepdims=True)
    normed = (last_rows * lax.rsqrt(meansq + 1e-05) * final_gain[None, :]).astype(jnp.bfloat16)
    logits = jnp.dot(normed, head_weight, preferred_element_type=jnp.float32)

    mixer_f32 = None
    for half in range(groups):
        part = jnp.dot(gated_parts[half], w_blocks[:, half].reshape(-1, width),
                       preferred_element_type=jnp.float32)
        mixer_f32 = part if mixer_f32 is None else mixer_f32 + part
    mixer = mixer_f32.astype(jnp.bfloat16)
    layer_out = (resid.astype(jnp.float32) + mixer.astype(jnp.float32)).astype(jnp.bfloat16)
    return (layer_out, logits)


def solution(mesh):
    placed = (
        P(("req", "seq"), None),
        P(("req", "seq"), None),
        P(("req", "seq"), None),
        P(("req", "seq"), None),
        P(),
        P(),
        P(),
        P(),
        P("req", "seq"),
        P("req", None),
        P(),
        P(None, ("req", "seq")),
        P("req", None),
    )
    return jax.shard_map(
        mixer_layer,
        mesh=mesh,
        in_specs=placed,
        out_specs=(P("req", "seq"), P(None, ("req", "seq"))),
        check_vma=False,
    )
```

```python
import jax
import jax.numpy as jnp
from jax import lax
from jax.sharding import PartitionSpec as P

HEAD_DIM = 64
NGROUPS = 8
STATE = 128


def split_halves(value):
    upper = value.astype(jnp.bfloat16)
    lower = (value - upper.astype(jnp.float32)).astype(jnp.bfloat16)
    return (upper, lower)


def group_inner(operands):
    cum_g, scores_g, inflow_g, x_g, allowed_mask = operands
    diff = cum_g[:, None, :] - cum_g[None, :, :]
    decay = jnp.where(allowed_mask[:, :, None], jnp.exp(jnp.minimum(diff, 0.0)), 0.0)
    weights = decay * scores_g[:, :, None] * inflow_g[None, :, :]
    upper, lower = split_halves(weights)
    first_part = jnp.einsum("tsk,skp->tkp", upper, x_g, preferred_element_type=jnp.float32)
    second_part = jnp.einsum("tsk,skp->tkp", lower, x_g, preferred_element_type=jnp.float32)
    return first_part + second_part


def block_terms(xb, bb, cb, dtb, segment, live, prev_seg, rate, d_skip, groups):
    rows = xb.shape[0]
    heads = rate.shape[0]
    per_group = heads // groups
    x4 = xb.reshape(rows, groups, per_group, HEAD_DIM)
    bmat = bb.reshape(rows, groups, STATE)
    cmat = cb.reshape(rows, groups, STATE)
    livef = live.astype(jnp.float32)
    cum = jnp.cumsum(-rate[None, :] * dtb, axis=0)
    inflow = dtb * livef[:, None]
    index = jnp.arange(rows, dtype=jnp.int32)
    allowed_mask = (segment[:, None] == segment[None, :]) & (index[:, None] >= index[None, :])
    scores = jnp.einsum("tgn,sgn->gts", cmat, bmat, preferred_element_type=jnp.float32)
    cum_g = cum.reshape(rows, groups, per_group).transpose(1, 0, 2)
    inflow_g = inflow.reshape(rows, groups, per_group).transpose(1, 0, 2)
    x_g = x4.transpose(1, 0, 2, 3)
    allowed_all = jnp.broadcast_to(allowed_mask[None], (groups, rows, rows))
    y_groups = lax.map(group_inner, (cum_g, scores, inflow_g, x_g, allowed_all))
    y_inner = y_groups.transpose(1, 0, 2, 3)
    skip = d_skip.reshape(1, groups, per_group, 1) * x4.astype(jnp.float32)
    last_seg = segment[rows - 1]
    tail = (
        jnp.exp(cum[rows - 1][None, :] - cum)
        * (segment == last_seg).astype(jnp.float32)[:, None]
        * inflow
    )
    scaled = tail.reshape(rows, groups, per_group, 1) * x4.astype(jnp.float32)
    upper, lower = split_halves(scaled)
    state = jnp.einsum("sgkp,sgn->gkpn", upper, bmat, preferred_element_type=jnp.float32)
    state = state + jnp.einsum("sgkp,sgn->gkpn", lower, bmat, preferred_element_type=jnp.float32)
    keep = jnp.exp(cum[rows - 1]) * (last_seg == prev_seg).astype(jnp.float32)
    carry_w = jnp.exp(cum) * (segment == prev_seg).astype(jnp.float32)[:, None]
    return (y_inner + skip, keep, state.reshape(heads, HEAD_DIM, STATE), carry_w, cmat)


def carry_term(arriving_vector, cmat, carry_w, groups):
    rows = cmat.shape[0]
    heads = arriving_vector.shape[0]
    per_group = heads // groups
    state4 = arriving_vector.reshape(groups, per_group, HEAD_DIM, STATE)
    upper, lower = split_halves(state4)
    y_carry = jnp.einsum("tgn,gkpn->tgkp", cmat, upper, preferred_element_type=jnp.float32)
    y_carry = y_carry + jnp.einsum(
        "tgn,gkpn->tgkp", cmat, lower, preferred_element_type=jnp.float32
    )
    return y_carry * carry_w.reshape(rows, groups, per_group, 1)


def gate_norm(y, zgate, norm_gain, groups):
    rows = y.shape[0]
    gated = y * jax.nn.silu(zgate.astype(jnp.float32))
    blocks = gated.reshape(rows, groups, -1)
    meansq = jnp.mean(blocks * blocks, axis=-1, keepdims=True)
    normed = (blocks * lax.rsqrt(meansq + 1e-05)).reshape(rows, -1) * norm_gain[None, :]
    return normed.astype(jnp.bfloat16)


def gather_by_shifts(value, axis):
    count, mine = lax.axis_size(axis), lax.axis_index(axis)
    parts = [value]
    for shift in range(1, count):
        pairs = [(i, (i + shift) % count) for i in range(count)]
        parts.append(lax.ppermute(value, axis, perm=pairs))
    order = (mine - jnp.arange(count, dtype=jnp.int32)) % count
    return jnp.take(jnp.stack(parts), order, axis=0)


def gather_by_doubling(value, axis):
    count, mine = lax.axis_size(axis), lax.axis_index(axis)
    acc = value[None]
    step = 1
    while step < count:
        pairs = [(i, i ^ step) for i in range(count)]
        other = lax.ppermute(acc, axis, perm=pairs)
        low = (mine // step) % 2 == 0
        acc = jnp.where(low, jnp.concatenate([acc, other]), jnp.concatenate([other, acc]))
        step *= 2
    return acc


def mixer_layer(
    xs,
    bc,
    zgate,
    dt_raw,
    dt_bias,
    a_log,
    d_skip,
    norm_gain,
    resid,
    w_out,
    final_gain,
    head_weight,
    lengths,
):
    rows = xs.shape[0]
    inner = xs.shape[1]
    seq_count = lax.axis_size("seq")
    place = lax.axis_index("seq")
    heads_all = a_log.shape[0]
    heads = heads_all // seq_count
    groups = NGROUPS // seq_count
    group_rows = rows * seq_count

    lens = lengths[0]
    slots = lens.shape[0]
    ends = jnp.cumsum(lens)
    positions = jnp.arange(group_rows, dtype=jnp.int32)
    segment = jnp.sum((positions[:, None] >= ends[None, :]).astype(jnp.int32), axis=1)
    live = segment < slots
    group_pos = jnp.arange(group_rows, dtype=jnp.int32)
    picker = (group_pos[None, :] == (ends - 1)[:, None]).astype(jnp.bfloat16)

    width = resid.shape[1]
    w_cols = lax.dynamic_slice_in_dim(w_out, place * width, width, axis=1)
    w_full = lax.all_gather(w_cols, "req", axis=0, tiled=True)
    w_blocks = w_full.reshape(seq_count, groups, inner // NGROUPS, width)

    block_cols = inner // NGROUPS
    block_heads = heads // groups

    def by_dest(part, width_of, half):
        piece = part.reshape(rows, seq_count, groups, width_of)[:, :, half, :]
        return piece.transpose(1, 0, 2)

    moves = []
    for half in range(groups):
        packed = jnp.concatenate(
            [
                by_dest(xs, block_cols, half),
                by_dest(zgate, block_cols, half),
                by_dest(bc[:, : NGROUPS * STATE], STATE, half),
                by_dest(bc[:, NGROUPS * STATE :], STATE, half),
                by_dest(dt_raw, block_heads, half),
            ],
            axis=2,
        )
        moves.append(lax.all_to_all(packed, "seq", split_axis=0, concat_axis=0, tiled=True))

    gated_parts = []
    picked_parts = []
    for half in range(groups):
        moved = moves[half]
        if half > 0:
            moved = lax.optimization_barrier((moved, gated))[0]
        moved = moved.reshape(group_rows, -1)
        xg = moved[:, :block_cols]
        zg = moved[:, block_cols : 2 * block_cols]
        bg = moved[:, 2 * block_cols : 2 * block_cols + STATE]
        cg = moved[:, 2 * block_cols + STATE : 2 * block_cols + 2 * STATE]
        dg = moved[:, 2 * block_cols + 2 * STATE :]

        first_head = (place * groups + half) * block_heads
        my_heads = lambda v: lax.dynamic_slice_in_dim(v, first_head, block_heads)
        rate = jnp.exp(my_heads(a_log))
        skipw = my_heads(d_skip)
        steps_dt = jax.nn.softplus(dg.astype(jnp.float32) + my_heads(dt_bias)[None, :])

        state_in = jnp.zeros((block_heads, HEAD_DIM, STATE), jnp.float32)
        prev_seg = jnp.array(-1, jnp.int32)
        ys = []
        for chunk in range(seq_count):
            lo, hi = chunk * rows, (chunk + 1) * rows
            local, keep, state, carry_w, cmat = block_terms(
                xg[lo:hi], bg[lo:hi], cg[lo:hi], steps_dt[lo:hi], segment[lo:hi], live[lo:hi],
                prev_seg, rate, skipw, 1,
            )
            y4 = (local + carry_term(state_in, cmat, carry_w, 1)) * live[lo:hi].astype(
                jnp.float32
            )[:, None, None, None]
            ys.append(y4.reshape(rows, block_cols))
            state_in = keep[:, None, None] * state_in + state
            prev_seg = segment[hi - 1]
        y = jnp.concatenate(ys, axis=0)
        gain = lax.dynamic_slice_in_dim(norm_gain, (place * groups + half) * block_cols, block_cols)
        gated = gate_norm(y, zg, gain, 1)
        gated_parts.append(lax.all_gather(gated, "seq", axis=1, tiled=True))
        picked_parts.append(
            jnp.dot(picker, gated, preferred_element_type=jnp.float32).astype(jnp.bfloat16)
        )

    picked_resid = jnp.dot(picker, resid, preferred_element_type=jnp.float32)
    picked = gather_by_shifts(jnp.stack(picked_parts, axis=1), "seq")
    picked_mixer = jnp.einsum("sthj,shjo->to", picked, w_blocks, preferred_element_type=jnp.float32)
    picked_rows = (
        picked_resid + picked_mixer.astype(jnp.bfloat16).astype(jnp.float32)
    ).astype(jnp.bfloat16)
    row_pair = gather_by_shifts(picked_rows, "seq").transpose(1, 0, 2).reshape(slots, -1)
    collected = gather_by_doubling(row_pair, "req")
    last_rows = collected.reshape(-1, seq_count * width).astype(jnp.float32)
    meansq = jnp.mean(last_rows * last_rows, axis=-1, keepdims=True)
    normed = (last_rows * lax.rsqrt(meansq + 1e-05) * final_gain[None, :]).astype(jnp.bfloat16)
    logits = jnp.dot(normed, head_weight, preferred_element_type=jnp.float32)

    mixer_f32 = None
    for half in range(groups):
        part = None
        for src in range(seq_count):
            cols = gated_parts[half][:, src * block_cols : (src + 1) * block_cols]
            piece = jnp.dot(cols, w_blocks[src, half], preferred_element_type=jnp.float32)
            part = piece if part is None else part + piece
        mixer_f32 = part if mixer_f32 is None else mixer_f32 + part
    mixer = mixer_f32.astype(jnp.bfloat16)
    layer_out = (resid.astype(jnp.float32) + mixer.astype(jnp.float32)).astype(jnp.bfloat16)
    return (layer_out, logits)


def solution(mesh):
    placed = (
        P(("req", "seq"), None),
        P(("req", "seq"), None),
        P(("req", "seq"), None),
        P(("req", "seq"), None),
        P(),
        P(),
        P(),
        P(),
        P("req", "seq"),
        P("req", None),
        P(),
        P(None, ("req", "seq")),
        P("req", None),
    )
    return jax.shard_map(
        mixer_layer,
        mesh=mesh,
        in_specs=placed,
        out_specs=(P("req", "seq"), P(None, ("req", "seq"))),
        check_vma=False,
    )
```

```python
import jax
import jax.numpy as jnp
from jax import lax
from jax.sharding import PartitionSpec as P

HEAD_DIM = 64
NGROUPS = 8
STATE = 128


def split_halves(value):
    upper = value.astype(jnp.bfloat16)
    lower = (value - upper.astype(jnp.float32)).astype(jnp.bfloat16)
    return (upper, lower)


def group_inner(operands):
    cum_g, scores_g, inflow_g, x_g, allowed_mask = operands
    diff = cum_g[:, None, :] - cum_g[None, :, :]
    decay = jnp.where(allowed_mask[:, :, None], jnp.exp(jnp.minimum(diff, 0.0)), 0.0)
    weights = decay * scores_g[:, :, None] * inflow_g[None, :, :]
    upper, lower = split_halves(weights)
    first_part = jnp.einsum("tsk,skp->tkp", upper, x_g, preferred_element_type=jnp.float32)
    second_part = jnp.einsum("tsk,skp->tkp", lower, x_g, preferred_element_type=jnp.float32)
    return first_part + second_part


def block_terms(xb, bb, cb, dtb, segment, live, prev_seg, rate, d_skip, groups):
    rows = xb.shape[0]
    heads = rate.shape[0]
    per_group = heads // groups
    x4 = xb.reshape(rows, groups, per_group, HEAD_DIM)
    bmat = bb.reshape(rows, groups, STATE)
    cmat = cb.reshape(rows, groups, STATE)
    livef = live.astype(jnp.float32)
    cum = jnp.cumsum(-rate[None, :] * dtb, axis=0)
    inflow = dtb * livef[:, None]
    index = jnp.arange(rows, dtype=jnp.int32)
    allowed_mask = (segment[:, None] == segment[None, :]) & (index[:, None] >= index[None, :])
    scores = jnp.einsum("tgn,sgn->gts", cmat, bmat, preferred_element_type=jnp.float32)
    cum_g = cum.reshape(rows, groups, per_group).transpose(1, 0, 2)
    inflow_g = inflow.reshape(rows, groups, per_group).transpose(1, 0, 2)
    x_g = x4.transpose(1, 0, 2, 3)
    allowed_all = jnp.broadcast_to(allowed_mask[None], (groups, rows, rows))
    y_groups = lax.map(group_inner, (cum_g, scores, inflow_g, x_g, allowed_all))
    y_inner = y_groups.transpose(1, 0, 2, 3)
    skip = d_skip.reshape(1, groups, per_group, 1) * x4.astype(jnp.float32)
    last_seg = segment[rows - 1]
    tail = (
        jnp.exp(cum[rows - 1][None, :] - cum)
        * (segment == last_seg).astype(jnp.float32)[:, None]
        * inflow
    )
    scaled = tail.reshape(rows, groups, per_group, 1) * x4.astype(jnp.float32)
    upper, lower = split_halves(scaled)
    state = jnp.einsum("sgkp,sgn->gkpn", upper, bmat, preferred_element_type=jnp.float32)
    state = state + jnp.einsum("sgkp,sgn->gkpn", lower, bmat, preferred_element_type=jnp.float32)
    keep = jnp.exp(cum[rows - 1]) * (last_seg == prev_seg).astype(jnp.float32)
    carry_w = jnp.exp(cum) * (segment == prev_seg).astype(jnp.float32)[:, None]
    return (y_inner + skip, keep, state.reshape(heads, HEAD_DIM, STATE), carry_w, cmat)


def carry_term(arriving_vector, cmat, carry_w, groups):
    rows = cmat.shape[0]
    heads = arriving_vector.shape[0]
    per_group = heads // groups
    state4 = arriving_vector.reshape(groups, per_group, HEAD_DIM, STATE)
    upper, lower = split_halves(state4)
    y_carry = jnp.einsum("tgn,gkpn->tgkp", cmat, upper, preferred_element_type=jnp.float32)
    y_carry = y_carry + jnp.einsum(
        "tgn,gkpn->tgkp", cmat, lower, preferred_element_type=jnp.float32
    )
    return y_carry * carry_w.reshape(rows, groups, per_group, 1)


def gate_norm(y, zgate, norm_gain, groups):
    rows = y.shape[0]
    gated = y * jax.nn.silu(zgate.astype(jnp.float32))
    blocks = gated.reshape(rows, groups, -1)
    meansq = jnp.mean(blocks * blocks, axis=-1, keepdims=True)
    normed = (blocks * lax.rsqrt(meansq + 1e-05)).reshape(rows, -1) * norm_gain[None, :]
    return normed.astype(jnp.bfloat16)


def gather_by_shifts(value, axis):
    count, mine = lax.axis_size(axis), lax.axis_index(axis)
    parts = [value]
    for shift in range(1, count):
        pairs = [(i, (i + shift) % count) for i in range(count)]
        parts.append(lax.ppermute(value, axis, perm=pairs))
    order = (mine - jnp.arange(count, dtype=jnp.int32)) % count
    return jnp.take(jnp.stack(parts), order, axis=0)


def all_to_all_by_shifts(value, axis):
    count, mine = lax.axis_size(axis), lax.axis_index(axis)
    parts = [lax.dynamic_index_in_dim(value, mine, 0, keepdims=False)]
    for shift in range(1, count):
        pairs = [(i, (i + shift) % count) for i in range(count)]
        piece = lax.dynamic_index_in_dim(value, (mine + shift) % count, 0, keepdims=False)
        parts.append(lax.ppermute(piece, axis, perm=pairs))
    chunks = []
    for source in range(count):
        shift = (mine - source) % count
        chunk = parts[0]
        for k in range(1, count):
            chunk = jnp.where(shift == k, parts[k], chunk)
        chunks.append(chunk)
    return jnp.stack(chunks)


def gather_by_doubling(value, axis):
    count, mine = lax.axis_size(axis), lax.axis_index(axis)
    acc = value[None]
    step = 1
    while step < count:
        pairs = [(i, i ^ step) for i in range(count)]
        other = lax.ppermute(acc, axis, perm=pairs)
        low = (mine // step) % 2 == 0
        acc = jnp.where(low, jnp.concatenate([acc, other]), jnp.concatenate([other, acc]))
        step *= 2
    return acc


def mixer_layer(
    xs,
    bc,
    zgate,
    dt_raw,
    dt_bias,
    a_log,
    d_skip,
    norm_gain,
    resid,
    w_out,
    final_gain,
    head_weight,
    lengths,
):
    rows = xs.shape[0]
    inner = xs.shape[1]
    seq_count = lax.axis_size("seq")
    place = lax.axis_index("seq")
    heads_all = a_log.shape[0]
    heads = heads_all // seq_count
    groups = NGROUPS // seq_count
    group_rows = rows * seq_count

    lens = lengths[0]
    slots = lens.shape[0]
    ends = jnp.cumsum(lens)
    positions = jnp.arange(group_rows, dtype=jnp.int32)
    segment = jnp.sum((positions[:, None] >= ends[None, :]).astype(jnp.int32), axis=1)
    live = segment < slots
    group_pos = jnp.arange(group_rows, dtype=jnp.int32)
    picker = (group_pos[None, :] == (ends - 1)[:, None]).astype(jnp.bfloat16)

    width = resid.shape[1]
    w_cols = lax.dynamic_slice_in_dim(w_out, place * width, width, axis=1)
    w_full = lax.all_gather(w_cols, "req", axis=0, tiled=True)
    w_blocks = w_full.reshape(seq_count, groups, inner // NGROUPS, width)

    block_cols = inner // NGROUPS
    block_heads = heads // groups

    def by_dest(part, width_of, half):
        piece = part.reshape(rows, seq_count, groups, width_of)[:, :, half, :]
        return piece.transpose(1, 0, 2)

    moves = []
    for half in range(groups):
        packed = jnp.concatenate(
            [
                by_dest(xs, block_cols, half),
                by_dest(zgate, block_cols, half),
                by_dest(bc[:, : NGROUPS * STATE], STATE, half),
                by_dest(bc[:, NGROUPS * STATE :], STATE, half),
                by_dest(dt_raw, block_heads, half),
            ],
            axis=2,
        )
        if moves:
            packed = lax.optimization_barrier((packed, moves[-1]))[0]
        moves.append(all_to_all_by_shifts(packed, "seq"))

    gated_parts = []
    picked_parts = []
    for half in range(groups):
        moved = moves[half]
        if half > 0:
            moved = lax.optimization_barrier((moved, gated))[0]
        moved = moved.reshape(group_rows, -1)
        xg = moved[:, :block_cols]
        zg = moved[:, block_cols : 2 * block_cols]
        bg = moved[:, 2 * block_cols : 2 * block_cols + STATE]
        cg = moved[:, 2 * block_cols + STATE : 2 * block_cols + 2 * STATE]
        dg = moved[:, 2 * block_cols + 2 * STATE :]

        first_head = (place * groups + half) * block_heads
        my_heads = lambda v: lax.dynamic_slice_in_dim(v, first_head, block_heads)
        rate = jnp.exp(my_heads(a_log))
        skipw = my_heads(d_skip)
        steps_dt = jax.nn.softplus(dg.astype(jnp.float32) + my_heads(dt_bias)[None, :])

        state_in = jnp.zeros((block_heads, HEAD_DIM, STATE), jnp.float32)
        prev_seg = jnp.array(-1, jnp.int32)
        ys = []
        for chunk in range(seq_count):
            lo, hi = chunk * rows, (chunk + 1) * rows
            local, keep, state, carry_w, cmat = block_terms(
                xg[lo:hi], bg[lo:hi], cg[lo:hi], steps_dt[lo:hi], segment[lo:hi], live[lo:hi],
                prev_seg, rate, skipw, 1,
            )
            y4 = (local + carry_term(state_in, cmat, carry_w, 1)) * live[lo:hi].astype(
                jnp.float32
            )[:, None, None, None]
            ys.append(y4.reshape(rows, block_cols))
            state_in = keep[:, None, None] * state_in + state
            prev_seg = segment[hi - 1]
        y = jnp.concatenate(ys, axis=0)
        gain = lax.dynamic_slice_in_dim(norm_gain, (place * groups + half) * block_cols, block_cols)
        gated = gate_norm(y, zg, gain, 1)
        gated_parts.append(lax.all_gather(gated, "seq", axis=1, tiled=True))
        picked_parts.append(
            jnp.dot(picker, gated, preferred_element_type=jnp.float32).astype(jnp.bfloat16)
        )

    picked_resid = jnp.dot(picker, resid, preferred_element_type=jnp.float32)
    picked = gather_by_shifts(jnp.stack(picked_parts, axis=1), "seq")
    picked_mixer = jnp.einsum("sthj,shjo->to", picked, w_blocks, preferred_element_type=jnp.float32)
    picked_rows = (
        picked_resid + picked_mixer.astype(jnp.bfloat16).astype(jnp.float32)
    ).astype(jnp.bfloat16)
    row_pair = gather_by_shifts(picked_rows, "seq").transpose(1, 0, 2).reshape(slots, -1)
    collected = gather_by_doubling(row_pair, "req")
    last_rows = collected.reshape(-1, seq_count * width).astype(jnp.float32)
    meansq = jnp.mean(last_rows * last_rows, axis=-1, keepdims=True)
    normed = (last_rows * lax.rsqrt(meansq + 1e-05) * final_gain[None, :]).astype(jnp.bfloat16)
    logits = jnp.dot(normed, head_weight, preferred_element_type=jnp.float32)

    mixer_f32 = None
    for half in range(groups):
        part = jnp.dot(gated_parts[half], w_blocks[:, half].reshape(-1, width),
                       preferred_element_type=jnp.float32)
        mixer_f32 = part if mixer_f32 is None else mixer_f32 + part
    mixer = mixer_f32.astype(jnp.bfloat16)
    layer_out = (resid.astype(jnp.float32) + mixer.astype(jnp.float32)).astype(jnp.bfloat16)
    return (layer_out, logits)


def solution(mesh):
    placed = (
        P(("req", "seq"), None),
        P(("req", "seq"), None),
        P(("req", "seq"), None),
        P(("req", "seq"), None),
        P(),
        P(),
        P(),
        P(),
        P("req", "seq"),
        P("req", None),
        P(),
        P(None, ("req", "seq")),
        P("req", None),
    )
    return jax.shard_map(
        mixer_layer,
        mesh=mesh,
        in_specs=placed,
        out_specs=(P("req", "seq"), P(None, ("req", "seq"))),
        check_vma=False,
    )
```

```python
import jax
import jax.numpy as jnp
from jax import lax
from jax.sharding import PartitionSpec as P

HEAD_DIM = 64
NGROUPS = 8
STATE = 128


def split_halves(value):
    upper = value.astype(jnp.bfloat16)
    lower = (value - upper.astype(jnp.float32)).astype(jnp.bfloat16)
    return (upper, lower)


def group_inner(operands):
    cum_g, scores_g, inflow_g, x_g, allowed_mask = operands
    diff = cum_g[:, None, :] - cum_g[None, :, :]
    decay = jnp.where(allowed_mask[:, :, None], jnp.exp(jnp.minimum(diff, 0.0)), 0.0)
    weights = decay * scores_g[:, :, None] * inflow_g[None, :, :]
    upper, lower = split_halves(weights)
    first_part = jnp.einsum("tsk,skp->tkp", upper, x_g, preferred_element_type=jnp.float32)
    second_part = jnp.einsum("tsk,skp->tkp", lower, x_g, preferred_element_type=jnp.float32)
    return first_part + second_part


def block_terms(xb, bb, cb, dtb, segment, live, prev_seg, rate, d_skip, groups):
    rows = xb.shape[0]
    heads = rate.shape[0]
    per_group = heads // groups
    x4 = xb.reshape(rows, groups, per_group, HEAD_DIM)
    bmat = bb.reshape(rows, groups, STATE)
    cmat = cb.reshape(rows, groups, STATE)
    livef = live.astype(jnp.float32)
    cum = jnp.cumsum(-rate[None, :] * dtb, axis=0)
    inflow = dtb * livef[:, None]
    index = jnp.arange(rows, dtype=jnp.int32)
    allowed_mask = (segment[:, None] == segment[None, :]) & (index[:, None] >= index[None, :])
    scores = jnp.einsum("tgn,sgn->gts", cmat, bmat, preferred_element_type=jnp.float32)
    cum_g = cum.reshape(rows, groups, per_group).transpose(1, 0, 2)
    inflow_g = inflow.reshape(rows, groups, per_group).transpose(1, 0, 2)
    x_g = x4.transpose(1, 0, 2, 3)
    allowed_all = jnp.broadcast_to(allowed_mask[None], (groups, rows, rows))
    y_groups = lax.map(group_inner, (cum_g, scores, inflow_g, x_g, allowed_all))
    y_inner = y_groups.transpose(1, 0, 2, 3)
    skip = d_skip.reshape(1, groups, per_group, 1) * x4.astype(jnp.float32)
    last_seg = segment[rows - 1]
    tail = (
        jnp.exp(cum[rows - 1][None, :] - cum)
        * (segment == last_seg).astype(jnp.float32)[:, None]
        * inflow
    )
    scaled = tail.reshape(rows, groups, per_group, 1) * x4.astype(jnp.float32)
    upper, lower = split_halves(scaled)
    state = jnp.einsum("sgkp,sgn->gkpn", upper, bmat, preferred_element_type=jnp.float32)
    state = state + jnp.einsum("sgkp,sgn->gkpn", lower, bmat, preferred_element_type=jnp.float32)
    keep = jnp.exp(cum[rows - 1]) * (last_seg == prev_seg).astype(jnp.float32)
    carry_w = jnp.exp(cum) * (segment == prev_seg).astype(jnp.float32)[:, None]
    return (y_inner + skip, keep, state.reshape(heads, HEAD_DIM, STATE), carry_w, cmat)


def carry_term(arriving_vector, cmat, carry_w, groups):
    rows = cmat.shape[0]
    heads = arriving_vector.shape[0]
    per_group = heads // groups
    state4 = arriving_vector.reshape(groups, per_group, HEAD_DIM, STATE)
    upper, lower = split_halves(state4)
    y_carry = jnp.einsum("tgn,gkpn->tgkp", cmat, upper, preferred_element_type=jnp.float32)
    y_carry = y_carry + jnp.einsum(
        "tgn,gkpn->tgkp", cmat, lower, preferred_element_type=jnp.float32
    )
    return y_carry * carry_w.reshape(rows, groups, per_group, 1)


def gate_norm(y, zgate, norm_gain, groups):
    rows = y.shape[0]
    gated = y * jax.nn.silu(zgate.astype(jnp.float32))
    blocks = gated.reshape(rows, groups, -1)
    meansq = jnp.mean(blocks * blocks, axis=-1, keepdims=True)
    normed = (blocks * lax.rsqrt(meansq + 1e-05)).reshape(rows, -1) * norm_gain[None, :]
    return normed.astype(jnp.bfloat16)


def gather_by_shifts(value, axis):
    count, mine = lax.axis_size(axis), lax.axis_index(axis)
    parts = [value]
    for shift in range(1, count):
        pairs = [(i, (i + shift) % count) for i in range(count)]
        parts.append(lax.ppermute(value, axis, perm=pairs))
    order = (mine - jnp.arange(count, dtype=jnp.int32)) % count
    return jnp.take(jnp.stack(parts), order, axis=0)


def gather_by_doubling(value, axis):
    count, mine = lax.axis_size(axis), lax.axis_index(axis)
    acc = value[None]
    step = 1
    while step < count:
        pairs = [(i, i ^ step) for i in range(count)]
        other = lax.ppermute(acc, axis, perm=pairs)
        low = (mine // step) % 2 == 0
        acc = jnp.where(low, jnp.concatenate([acc, other]), jnp.concatenate([other, acc]))
        step *= 2
    return acc


def mixer_layer(
    xs,
    bc,
    zgate,
    dt_raw,
    dt_bias,
    a_log,
    d_skip,
    norm_gain,
    resid,
    w_out,
    final_gain,
    head_weight,
    lengths,
):
    rows = xs.shape[0]
    inner = xs.shape[1]
    seq_count = lax.axis_size("seq")
    place = lax.axis_index("seq")
    heads_all = a_log.shape[0]
    heads = heads_all // seq_count
    groups = NGROUPS // seq_count
    group_rows = rows * seq_count

    lens = lengths[0]
    slots = lens.shape[0]
    ends = jnp.cumsum(lens)
    positions = jnp.arange(group_rows, dtype=jnp.int32)
    segment = jnp.sum((positions[:, None] >= ends[None, :]).astype(jnp.int32), axis=1)
    live = segment < slots
    group_pos = jnp.arange(group_rows, dtype=jnp.int32)
    picker = (group_pos[None, :] == (ends - 1)[:, None]).astype(jnp.bfloat16)

    width = resid.shape[1]
    w_cols = lax.dynamic_slice_in_dim(w_out, place * width, width, axis=1)
    w_full = lax.all_gather(w_cols, "req", axis=0, tiled=True)
    w_blocks = w_full.reshape(groups, seq_count, inner // NGROUPS, width)

    block_cols = inner // NGROUPS
    block_heads = heads // groups

    def by_dest(part, width_of, half):
        piece = part.reshape(rows, groups, seq_count, width_of)[:, half, :, :]
        return piece.transpose(1, 0, 2)

    moves = []
    for half in range(groups):
        packed = jnp.concatenate(
            [
                by_dest(xs, block_cols, half),
                by_dest(zgate, block_cols, half),
                by_dest(bc[:, : NGROUPS * STATE], STATE, half),
                by_dest(bc[:, NGROUPS * STATE :], STATE, half),
                by_dest(dt_raw, block_heads, half),
            ],
            axis=2,
        )
        moves.append(lax.all_to_all(packed, "seq", split_axis=0, concat_axis=0, tiled=True))

    gated_parts = []
    picked_parts = []
    for half in range(groups):
        moved = moves[half]
        if half > 0:
            moved = lax.optimization_barrier((moved, gated))[0]
        moved = moved.reshape(group_rows, -1)
        xg = moved[:, :block_cols]
        zg = moved[:, block_cols : 2 * block_cols]
        bg = moved[:, 2 * block_cols : 2 * block_cols + STATE]
        cg = moved[:, 2 * block_cols + STATE : 2 * block_cols + 2 * STATE]
        dg = moved[:, 2 * block_cols + 2 * STATE :]

        first_head = (half * seq_count + place) * block_heads
        my_heads = lambda v: lax.dynamic_slice_in_dim(v, first_head, block_heads)
        rate = jnp.exp(my_heads(a_log))
        skipw = my_heads(d_skip)
        steps_dt = jax.nn.softplus(dg.astype(jnp.float32) + my_heads(dt_bias)[None, :])

        state_in = jnp.zeros((block_heads, HEAD_DIM, STATE), jnp.float32)
        prev_seg = jnp.array(-1, jnp.int32)
        ys = []
        for chunk in range(seq_count):
            lo, hi = chunk * rows, (chunk + 1) * rows
            local, keep, state, carry_w, cmat = block_terms(
                xg[lo:hi], bg[lo:hi], cg[lo:hi], steps_dt[lo:hi], segment[lo:hi], live[lo:hi],
                prev_seg, rate, skipw, 1,
            )
            y4 = (local + carry_term(state_in, cmat, carry_w, 1)) * live[lo:hi].astype(
                jnp.float32
            )[:, None, None, None]
            ys.append(y4.reshape(rows, block_cols))
            state_in = keep[:, None, None] * state_in + state
            prev_seg = segment[hi - 1]
        y = jnp.concatenate(ys, axis=0)
        gain = lax.dynamic_slice_in_dim(norm_gain, (half * seq_count + place) * block_cols, block_cols)
        gated = gate_norm(y, zg, gain, 1)
        gated_parts.append(lax.all_gather(gated, "seq", axis=1, tiled=True))
        picked_parts.append(
            jnp.dot(picker, gated, preferred_element_type=jnp.float32).astype(jnp.bfloat16)
        )

    picked_resid = jnp.dot(picker, resid, preferred_element_type=jnp.float32)
    picked = gather_by_shifts(jnp.stack(picked_parts, axis=1), "seq")
    picked_mixer = jnp.einsum("sthj,hsjo->to", picked, w_blocks, preferred_element_type=jnp.float32)
    picked_rows = (
        picked_resid + picked_mixer.astype(jnp.bfloat16).astype(jnp.float32)
    ).astype(jnp.bfloat16)
    row_pair = gather_by_shifts(picked_rows, "seq").transpose(1, 0, 2).reshape(slots, -1)
    collected = gather_by_doubling(row_pair, "req")
    last_rows = collected.reshape(-1, seq_count * width).astype(jnp.float32)
    meansq = jnp.mean(last_rows * last_rows, axis=-1, keepdims=True)
    normed = (last_rows * lax.rsqrt(meansq + 1e-05) * final_gain[None, :]).astype(jnp.bfloat16)
    logits = jnp.dot(normed, head_weight, preferred_element_type=jnp.float32)

    mixer_f32 = None
    for half in range(groups):
        part = jnp.dot(gated_parts[half], w_blocks[half].reshape(-1, width),
                       preferred_element_type=jnp.float32)
        mixer_f32 = part if mixer_f32 is None else mixer_f32 + part
    mixer = mixer_f32.astype(jnp.bfloat16)
    layer_out = (resid.astype(jnp.float32) + mixer.astype(jnp.float32)).astype(jnp.bfloat16)
    return (layer_out, logits)


def solution(mesh):
    placed = (
        P(("req", "seq"), None),
        P(("req", "seq"), None),
        P(("req", "seq"), None),
        P(("req", "seq"), None),
        P(),
        P(),
        P(),
        P(),
        P("req", "seq"),
        P("req", None),
        P(),
        P(None, ("req", "seq")),
        P("req", None),
    )
    return jax.shard_map(
        mixer_layer,
        mesh=mesh,
        in_specs=placed,
        out_specs=(P("req", "seq"), P(None, ("req", "seq"))),
        check_vma=False,
    )
```

```python
import jax
import jax.numpy as jnp
from jax import lax
from jax.sharding import PartitionSpec as P

HEAD_DIM = 64
NGROUPS = 8
STATE = 128


def split_halves(value):
    upper = value.astype(jnp.bfloat16)
    lower = (value - upper.astype(jnp.float32)).astype(jnp.bfloat16)
    return (upper, lower)


def group_inner(operands):
    cum_g, scores_g, inflow_g, x_g, allowed_mask = operands
    diff = cum_g[:, None, :] - cum_g[None, :, :]
    decay = jnp.where(allowed_mask[:, :, None], jnp.exp(jnp.minimum(diff, 0.0)), 0.0)
    weights = decay * scores_g[:, :, None] * inflow_g[None, :, :]
    upper, lower = split_halves(weights)
    first_part = jnp.einsum("tsk,skp->tkp", upper, x_g, preferred_element_type=jnp.float32)
    second_part = jnp.einsum("tsk,skp->tkp", lower, x_g, preferred_element_type=jnp.float32)
    return first_part + second_part


def block_terms(xb, bb, cb, dtb, segment, live, prev_seg, rate, d_skip, groups):
    rows = xb.shape[0]
    heads = rate.shape[0]
    per_group = heads // groups
    x4 = xb.reshape(rows, groups, per_group, HEAD_DIM)
    bmat = bb.reshape(rows, groups, STATE)
    cmat = cb.reshape(rows, groups, STATE)
    livef = live.astype(jnp.float32)
    cum = jnp.cumsum(-rate[None, :] * dtb, axis=0)
    inflow = dtb * livef[:, None]
    index = jnp.arange(rows, dtype=jnp.int32)
    allowed_mask = (segment[:, None] == segment[None, :]) & (index[:, None] >= index[None, :])
    scores = jnp.einsum("tgn,sgn->gts", cmat, bmat, preferred_element_type=jnp.float32)
    cum_g = cum.reshape(rows, groups, per_group).transpose(1, 0, 2)
    inflow_g = inflow.reshape(rows, groups, per_group).transpose(1, 0, 2)
    x_g = x4.transpose(1, 0, 2, 3)
    allowed_all = jnp.broadcast_to(allowed_mask[None], (groups, rows, rows))
    y_groups = lax.map(group_inner, (cum_g, scores, inflow_g, x_g, allowed_all))
    y_inner = y_groups.transpose(1, 0, 2, 3)
    skip = d_skip.reshape(1, groups, per_group, 1) * x4.astype(jnp.float32)
    last_seg = segment[rows - 1]
    tail = (
        jnp.exp(cum[rows - 1][None, :] - cum)
        * (segment == last_seg).astype(jnp.float32)[:, None]
        * inflow
    )
    scaled = tail.reshape(rows, groups, per_group, 1) * x4.astype(jnp.float32)
    upper, lower = split_halves(scaled)
    state = jnp.einsum("sgkp,sgn->gkpn", upper, bmat, preferred_element_type=jnp.float32)
    state = state + jnp.einsum("sgkp,sgn->gkpn", lower, bmat, preferred_element_type=jnp.float32)
    keep = jnp.exp(cum[rows - 1]) * (last_seg == prev_seg).astype(jnp.float32)
    carry_w = jnp.exp(cum) * (segment == prev_seg).astype(jnp.float32)[:, None]
    return (y_inner + skip, keep, state.reshape(heads, HEAD_DIM, STATE), carry_w, cmat)


def carry_term(arriving_vector, cmat, carry_w, groups):
    rows = cmat.shape[0]
    heads = arriving_vector.shape[0]
    per_group = heads // groups
    state4 = arriving_vector.reshape(groups, per_group, HEAD_DIM, STATE)
    upper, lower = split_halves(state4)
    y_carry = jnp.einsum("tgn,gkpn->tgkp", cmat, upper, preferred_element_type=jnp.float32)
    y_carry = y_carry + jnp.einsum(
        "tgn,gkpn->tgkp", cmat, lower, preferred_element_type=jnp.float32
    )
    return y_carry * carry_w.reshape(rows, groups, per_group, 1)


def gate_norm(y, zgate, norm_gain, groups):
    rows = y.shape[0]
    gated = y * jax.nn.silu(zgate.astype(jnp.float32))
    blocks = gated.reshape(rows, groups, -1)
    meansq = jnp.mean(blocks * blocks, axis=-1, keepdims=True)
    normed = (blocks * lax.rsqrt(meansq + 1e-05)).reshape(rows, -1) * norm_gain[None, :]
    return normed.astype(jnp.bfloat16)


def gather_by_shifts(value, axis):
    count, mine = lax.axis_size(axis), lax.axis_index(axis)
    parts = [value]
    for shift in range(1, count):
        pairs = [(i, (i + shift) % count) for i in range(count)]
        parts.append(lax.ppermute(value, axis, perm=pairs))
    order = (mine - jnp.arange(count, dtype=jnp.int32)) % count
    return jnp.take(jnp.stack(parts), order, axis=0)


def gather_by_doubling(value, axis):
    count, mine = lax.axis_size(axis), lax.axis_index(axis)
    acc = value[None]
    step = 1
    while step < count:
        pairs = [(i, i ^ step) for i in range(count)]
        other = lax.ppermute(acc, axis, perm=pairs)
        low = (mine // step) % 2 == 0
        acc = jnp.where(low, jnp.concatenate([acc, other]), jnp.concatenate([other, acc]))
        step *= 2
    return acc


def mixer_layer(
    xs,
    bc,
    zgate,
    dt_raw,
    dt_bias,
    a_log,
    d_skip,
    norm_gain,
    resid,
    w_out,
    final_gain,
    head_weight,
    lengths,
):
    rows = xs.shape[0]
    inner = xs.shape[1]
    seq_count = lax.axis_size("seq")
    place = lax.axis_index("seq")
    heads_all = a_log.shape[0]
    heads = heads_all // seq_count
    groups = NGROUPS // seq_count
    group_rows = rows * seq_count

    lens = lengths[0]
    slots = lens.shape[0]
    ends = jnp.cumsum(lens)
    positions = jnp.arange(group_rows, dtype=jnp.int32)
    segment = jnp.sum((positions[:, None] >= ends[None, :]).astype(jnp.int32), axis=1)
    live = segment < slots
    group_pos = jnp.arange(group_rows, dtype=jnp.int32)
    picker = (group_pos[None, :] == (ends - 1)[:, None]).astype(jnp.bfloat16)

    width = resid.shape[1]
    w_cols = lax.dynamic_slice_in_dim(w_out, place * width, width, axis=1)
    w_full = lax.all_gather(w_cols, "req", axis=0, tiled=True)
    w_blocks = w_full.reshape(groups, seq_count, inner // NGROUPS, width)

    block_cols = inner // NGROUPS
    block_heads = heads // groups

    def by_dest(part, width_of, half):
        piece = part.reshape(rows, groups, seq_count, width_of)[:, half, :, :]
        return piece.transpose(1, 0, 2)

    moves = []
    for half in range(groups):
        packed = jnp.concatenate(
            [
                by_dest(xs, block_cols, half),
                by_dest(zgate, block_cols, half),
                by_dest(bc[:, : NGROUPS * STATE], STATE, half),
                by_dest(bc[:, NGROUPS * STATE :], STATE, half),
                by_dest(dt_raw, block_heads, half),
            ],
            axis=2,
        )
        moves.append(lax.all_to_all(packed, "seq", split_axis=0, concat_axis=0, tiled=True))

    gated_parts = []
    picked_parts = []
    for half in range(groups):
        moved = moves[half]
        if half > 0:
            moved = lax.optimization_barrier((moved, gated))[0]
        moved = moved.reshape(group_rows, -1)
        xg = moved[:, :block_cols]
        zg = moved[:, block_cols : 2 * block_cols]
        bg = moved[:, 2 * block_cols : 2 * block_cols + STATE]
        cg = moved[:, 2 * block_cols + STATE : 2 * block_cols + 2 * STATE]
        dg = moved[:, 2 * block_cols + 2 * STATE :]

        first_head = (half * seq_count + place) * block_heads
        my_heads = lambda v: lax.dynamic_slice_in_dim(v, first_head, block_heads)
        rate = jnp.exp(my_heads(a_log))
        skipw = my_heads(d_skip)
        steps_dt = jax.nn.softplus(dg.astype(jnp.float32) + my_heads(dt_bias)[None, :])

        state_in = jnp.zeros((block_heads, HEAD_DIM, STATE), jnp.float32)
        prev_seg = jnp.array(-1, jnp.int32)
        ys = []
        for chunk in range(seq_count):
            lo, hi = chunk * rows, (chunk + 1) * rows
            local, keep, state, carry_w, cmat = block_terms(
                xg[lo:hi], bg[lo:hi], cg[lo:hi], steps_dt[lo:hi], segment[lo:hi], live[lo:hi],
                prev_seg, rate, skipw, 1,
            )
            y4 = (local + carry_term(state_in, cmat, carry_w, 1)) * live[lo:hi].astype(
                jnp.float32
            )[:, None, None, None]
            ys.append(y4.reshape(rows, block_cols))
            state_in = keep[:, None, None] * state_in + state
            prev_seg = segment[hi - 1]
        y = jnp.concatenate(ys, axis=0)
        gain = lax.dynamic_slice_in_dim(norm_gain, (half * seq_count + place) * block_cols, block_cols)
        gated = gate_norm(y, zg, gain, 1)
        gated_parts.append(lax.all_gather(gated, "seq", axis=1, tiled=True))
        picked_parts.append(
            jnp.dot(picker, gated, preferred_element_type=jnp.float32).astype(jnp.bfloat16)
        )

    picked_resid = jnp.dot(picker, resid, preferred_element_type=jnp.float32)
    picked = gather_by_shifts(jnp.stack(picked_parts, axis=1), "seq")
    picked_mixer = jnp.einsum("sthj,hsjo->to", picked, w_blocks, preferred_element_type=jnp.float32)
    picked_rows = (
        picked_resid + picked_mixer.astype(jnp.bfloat16).astype(jnp.float32)
    ).astype(jnp.bfloat16)
    row_pair = gather_by_shifts(picked_rows, "seq").transpose(1, 0, 2).reshape(slots, -1)
    collected = gather_by_doubling(row_pair, "req")
    last_rows = collected.reshape(-1, seq_count * width).astype(jnp.float32)
    meansq = jnp.mean(last_rows * last_rows, axis=-1, keepdims=True)
    normed = (last_rows * lax.rsqrt(meansq + 1e-05) * final_gain[None, :]).astype(jnp.bfloat16)
    logits = jnp.dot(normed, head_weight, preferred_element_type=jnp.float32)

    mixer_f32 = None
    for half in range(groups):
        part = jnp.dot(gated_parts[half], w_blocks[half].reshape(-1, width),
                       preferred_element_type=jnp.float32)
        if mixer_f32 is None:
            mixer_f32 = lax.optimization_barrier(part)
        else:
            mixer_f32 = mixer_f32 + part
    mixer = mixer_f32.astype(jnp.bfloat16)
    layer_out = (resid.astype(jnp.float32) + mixer.astype(jnp.float32)).astype(jnp.bfloat16)
    return (layer_out, logits)


def solution(mesh):
    placed = (
        P(("req", "seq"), None),
        P(("req", "seq"), None),
        P(("req", "seq"), None),
        P(("req", "seq"), None),
        P(),
        P(),
        P(),
        P(),
        P("req", "seq"),
        P("req", None),
        P(),
        P(None, ("req", "seq")),
        P("req", None),
    )
    return jax.shard_map(
        mixer_layer,
        mesh=mesh,
        in_specs=placed,
        out_specs=(P("req", "seq"), P(None, ("req", "seq"))),
        check_vma=False,
    )
```
